256 devices in a mesh: band: 2 (over y_hi), domain: 128 (over y_lo, x, z, core).
Axes of the slice: x: 4, y: 4 (y_hi: 2, y_lo: 2; y = y_hi * 2 + y_lo), z: 8, core: 2. Of those that a mesh axis runs over, the one named last changes fastest.
Arguments:
- targets: float32 [4, 36864, 192], P('band', 'domain'), may hold values from -5 to 5
- partner_pool: bfloat16 [64, 36864, 192], P('band', 'domain'), may hold values from -5 to 5
- owners: int32 [2], replicated, may hold values from 0 to 1, as said below
- warm_start: bfloat16 [2, 8, 4, 36864, 192], P(None, None, 'band', 'domain'), may hold values from -6 to 6
Outputs:
- exchange: float32 [4, 36864, 192], P('band', 'domain')
The draws below stay inside these ranges and needn't reach their ends.
Inputs may be any that keep to these rules, and one draw needn't show every extreme that they name: The 2 broadcast blocks have distinct owners.
All inputs are finite; a program needn't handle non-finite values.
Results may differ from the reference program's by a relative error of at most 0.0006.
Values may be sent and summed in bfloat16 or wider, within the bound.
No kernel may reach another device: no remote copies, remote signals or barrier semaphores. Data moves between devices by JAX's collectives and lax.ppermute only.
A program may use at most 192 MiB of HBM per device.

```python
import math
import jax
import jax.numpy as jnp
from jax import lax

ORB = 8
POOL = 4
STEPS = 2
SWEEPS = 3
TGT = 2
GX = 192
GY = 192
GZ = 192
GROUPS = 2


def orbital_field(key, row_count):
    key_jitter, key_offset = jax.random.split(key, 2)
    position = (jnp.arange(GX * GY, dtype=jnp.int32) // GY).astype(jnp.float32) / GX
    jitter = jnp.clip(jax.random.normal(key_jitter, (row_count, GX * GY, GZ), jnp.float32), -5.0, 5.0)
    offset = jax.random.uniform(key_offset, (row_count, 1, 1), jnp.float32, -0.8, 0.8)
    envelope = 0.5 + position
    return 0.5 * envelope[None, :, None] * (offset + jitter)


def draw_targets(key, part):
    return orbital_field(jax.random.fold_in(key, 11), GROUPS * TGT)


def draw_partner_pool(key, part):
    return orbital_field(jax.random.fold_in(key, 23), GROUPS * POOL * ORB).astype(jnp.bfloat16)


def draw_owners(key, part):
    shuffled = jax.random.permutation(jax.random.fold_in(key, 37), jnp.arange(GROUPS, dtype=jnp.int32))
    return shuffled[:STEPS]


def steps_of(own_key, shape, shards, smallest, high):
    level = 1.0
    for dim, blocks in shards:
        heights = jax.random.uniform(jax.random.fold_in(jax.random.fold_in(own_key, 6), dim), (blocks,), jnp.float32, smallest / len(shards), high / len(shards))
        level = level * jnp.repeat(jnp.exp(heights), shape[dim] // blocks).reshape((-1,) + (1,) * (len(shape) - 1 - dim))
    return level


def gaussian(own_key, extent, width, limit, shards=(), kind=jnp.bfloat16):
    factor_of = steps_of(own_key, extent, shards, -0.22, 0.18) if shards else 1.0
    values = jax.random.normal(own_key, extent, jnp.float32) * width * factor_of
    return jnp.minimum(jnp.maximum(values, -limit), limit).astype(kind)


def setup_inputs(seed: int = 0) -> dict:
    key_of = jax.random.split(jax.random.key(seed), 5)
    targets = draw_targets(jax.random.fold_in(key_of[4], 71), 0)
    partner_pool = draw_partner_pool(jax.random.fold_in(key_of[4], 71), 0)
    owners = draw_owners(jax.random.fold_in(key_of[4], 71), 0)
    warm_start = gaussian(key_of[3], (STEPS, ORB, GROUPS * TGT, GX * GY, GZ), 1.0, 6.0, ((2, 2), (3, 128)))
    return dict(targets=targets, partner_pool=partner_pool, owners=owners, warm_start=warm_start)


coupling = 4.0 * math.pi


def jacobi(potential, source):
    beside = jnp.roll(potential, 1, 1) + jnp.roll(potential, -1, 1)
    beside = beside + jnp.roll(potential, 1, 2) + jnp.roll(potential, -1, 2)
    beside = beside + jnp.roll(potential, 1, 3) + jnp.roll(potential, -1, 3)
    return (beside + coupling * source) / 6.0


def reference(targets, partner_pool, owners, warm_start):
    grid_shape = (GX, GY, GZ)
    cell_count = GX * GY * GZ
    exchange = jnp.zeros(targets.shape, jnp.float32)
    for block_index in range(STEPS):
        first_row = (owners[block_index] * POOL + block_index) * ORB
        partner = lax.dynamic_slice_in_dim(partner_pool, first_row.astype(jnp.int32), ORB, 0)
        partner = partner.astype(jnp.float32).reshape((ORB,) + grid_shape)
        warm_block = warm_start[block_index]

        def one_target(target_index):
            target = lax.dynamic_index_in_dim(targets, target_index, 0, keepdims=False).reshape(grid_shape)
            start_field = lax.dynamic_index_in_dim(warm_block, target_index, 1, keepdims=False)
            start_field = start_field.reshape((ORB,) + grid_shape)
            density = partner * target[None]
            mean_value = jnp.sum(density, axis=(1, 2, 3), keepdims=True) / cell_count
            source = density - mean_value
            potential = start_field.astype(jnp.float32)
            for sweep_index in range(SWEEPS):
                potential = jacobi(potential, source)
            return jnp.sum(potential * partner, axis=0).reshape(targets.shape[1:])

        contribution = lax.map(one_target, jnp.arange(GROUPS * TGT, dtype=jnp.int32))
        exchange = exchange - contribution
    return exchange
```

```python
import functools
import math

import jax
import jax.numpy as jnp
from jax import lax
from jax.experimental import pallas as pl
from jax.experimental.pallas import tpu as pltpu
from jax.sharding import PartitionSpec as P

ORB = 8
STEPS = 2
SWEEPS = 3
GX = 192
GY = 192
GZ = 192


coupling = 4.0 * math.pi
OFFLOAD_WIDTH = 16384


def circulant(width):
    a = lax.broadcasted_iota(jnp.int32, (width, width), 0)
    b = lax.broadcasted_iota(jnp.int32, (width, width), 1)
    gap = (a - b + width) % width
    return ((gap == 1) | (gap == width - 1)).astype(jnp.bfloat16)


def stencil(y0, v, lo, hi, q, t_ref, wide):
    row_count = v.shape[0]
    halo = lo.shape[0]
    wide[0:halo, :] = lo
    wide[halo : halo + row_count, :] = v
    wide[halo + row_count : 2 * halo + row_count, :] = hi
    beside = wide[0:row_count, :] + wide[2 * halo : 2 * halo + row_count, :]
    down = wide[halo - 1 : halo - 1 + row_count, :]
    up = wide[halo + 1 : halo + 1 + row_count, :]
    down_wrap = wide[2 * halo - 1 : 2 * halo - 1 + row_count, :]
    up_wrap = wide[1 : 1 + row_count, :]
    y = lax.broadcasted_iota(jnp.int32, v.shape, 0) + y0
    for _ in range((row_count + GY - 2) // GY):
        y = jnp.where(y >= GY, y - GY, y)
    beside = beside + jnp.where(y == 0, down_wrap, down)
    beside = beside + jnp.where(y == GY - 1, up_wrap, up)
    high = v.astype(jnp.bfloat16)
    low = (v - high.astype(jnp.float32)).astype(jnp.bfloat16)
    tmat = t_ref[...]
    beside = beside + jnp.dot(high, tmat, preferred_element_type=jnp.float32)
    beside = beside + jnp.dot(low, tmat, preferred_element_type=jnp.float32)
    return (beside + coupling * q) * (1.0 / 6.0)


def sweep_kernel(final, sc_ref, v_ref, lo_ref, hi_ref, p_ref, t_ref, c_ref, *rest):
    y0 = sc_ref[0]
    part = p_ref[...].astype(jnp.float32)
    row_count = part.shape[0]
    halo = lo_ref.shape[-2]
    if final:
        acc_ref, wide = rest

        @pl.when(pl.program_id(0) == 0)
        def _():
            acc_ref[...] = jnp.zeros_like(acc_ref)

    else:
        out_ref, fwd_ref, bwd_ref, wide = rest
    for j in range(v_ref.shape[0]):
        q = part * t_ref[j]
        new = stencil(
            y0,
            v_ref[j].astype(jnp.float32),
            lo_ref[j].astype(jnp.float32),
            hi_ref[j].astype(jnp.float32),
            q,
            c_ref,
            wide,
        )
        if final:
            acc_ref[j] = acc_ref[j] + new * part
        else:
            out_ref[j] = new
            fwd_ref[j] = new[row_count - halo : row_count].astype(jnp.bfloat16)
            bwd_ref[j] = new[0:halo].astype(jnp.bfloat16)


def sweep_call(final, v, from_warm, lo, hi, partner, targets, tmat, scalars):
    orb, tgt, halo, width = lo.shape
    row_count = targets.shape[1]
    if from_warm:
        v_spec = pl.BlockSpec(
            (None, None, tgt, row_count, width), lambda i, sc: (sc[1], i, 0, 0, 0)
        )
    else:
        v_spec = pl.BlockSpec((None, tgt, row_count, width), lambda i, sc: (i, 0, 0, 0))
    h_spec = pl.BlockSpec((None, tgt, halo, width), lambda i, sc: (i, 0, 0, 0))
    p_spec = pl.BlockSpec((None, row_count, width), lambda i, sc: (sc[2] + i, 0, 0))
    t_spec = pl.BlockSpec((tgt, row_count, width), lambda i, sc: (0, 0, 0))
    c_spec = pl.BlockSpec((width, width), lambda i, sc: (0, 0))
    cells = orb * tgt * row_count * width
    if final:
        out_shape = jax.ShapeDtypeStruct((tgt, row_count, width), jnp.float32)
        out_specs = pl.BlockSpec((tgt, row_count, width), lambda i, sc: (0, 0, 0))
        out_bytes = tgt * row_count * width * 4
    else:
        out_shape = (
            jax.ShapeDtypeStruct((orb, tgt, row_count, width), jnp.float32),
            jax.ShapeDtypeStruct((orb, tgt, halo, width), jnp.bfloat16),
            jax.ShapeDtypeStruct((orb, tgt, halo, width), jnp.bfloat16),
        )
        out_specs = (
            pl.BlockSpec((None, tgt, row_count, width), lambda i, sc: (i, 0, 0, 0)),
            h_spec,
            h_spec,
        )
        out_bytes = cells * 4 + 2 * orb * tgt * halo * width * 2
    in_bytes = (
        cells * v.dtype.itemsize
        + 2 * orb * tgt * halo * width * 2
        + orb * row_count * width * 2
        + tgt * row_count * width * 4
    )
    grid_spec = pltpu.PrefetchScalarGridSpec(
        num_scalar_prefetch=1,
        grid=(orb,),
        in_specs=[v_spec, h_spec, h_spec, p_spec, t_spec, c_spec],
        out_specs=out_specs,
        scratch_shapes=[pltpu.VMEM((row_count + 2 * halo, width), jnp.float32)],
    )
    return pl.pallas_call(
        functools.partial(sweep_kernel, final),
        grid_spec=grid_spec,
        out_shape=out_shape,
        compiler_params=pltpu.CompilerParams(dimension_semantics=("arbitrary",)),
        cost_estimate=pl.CostEstimate(
            flops=cells * (4 * width + 24),
            transcendentals=0,
            bytes_accessed=in_bytes + out_bytes,
        ),
    )(scalars, v, lo, hi, partner, targets, tmat)


def exchange_halos(fwd, bwd):
    count = lax.axis_size("domain")
    forward = [(k, (k + 1) % count) for k in range(count)]
    backward = [((k + 1) % count, k) for k in range(count)]
    return lax.ppermute(fwd, "domain", forward), lax.ppermute(bwd, "domain", backward)


def solve_stream(warm_start, s, partner, pbase, targets, tmat, y0):
    row_count = targets.shape[1]
    halo = GY
    warm_block = lax.dynamic_index_in_dim(warm_start, s, 0, keepdims=False)
    lo, hi = exchange_halos(
        warm_block[:, :, row_count - halo :], warm_block[:, :, :halo]
    )
    scalars = jnp.stack([y0, s, pbase]).astype(jnp.int32)
    potential, fwd, bwd = sweep_call(
        False, warm_start, True, lo, hi, partner, targets, tmat, scalars
    )
    for sweep_index in range(1, SWEEPS - 1):
        lo, hi = exchange_halos(fwd, bwd)
        potential, fwd, bwd = sweep_call(
            False, potential, False, lo, hi, partner, targets, tmat, scalars
        )
    lo, hi = exchange_halos(fwd, bwd)
    return sweep_call(True, potential, False, lo, hi, partner, targets, tmat, scalars)


def pair_sums(block, targets):
    part = block.astype(jnp.float32)
    return jnp.sum(part[:, None] * targets[None], axis=(2, 3))


def mean_term(block, means):
    part = block.astype(jnp.float32)
    total = None
    for i in range(block.shape[0]):
        term = means[i][:, None, None] * part[i][None]
        total = term if total is None else total + term
    return total


def body(targets, partner_pool, owners, warm_start):
    row_count = targets.shape[1]
    cell_count = GX * GY * GZ
    domain = lax.axis_index("domain")
    band = lax.axis_index("band")
    y0 = (domain * row_count) % GY
    s_own = jnp.where(owners[0] == band, 0, 1).astype(jnp.int32)
    s_rem = 1 - s_own
    own_block = lax.dynamic_slice_in_dim(partner_pool, s_own * ORB, ORB, 0)
    rem_block = lax.ppermute(own_block, "band", [(0, 1), (1, 0)])
    tmat = circulant(targets.shape[2])
    zero = jnp.zeros((), jnp.int32)

    sums = jnp.stack([pair_sums(own_block, targets), pair_sums(rem_block, targets)])
    padded = jnp.zeros((OFFLOAD_WIDTH,), jnp.float32).at[: sums.size].set(sums.reshape(-1))
    totals = lax.psum(padded, "domain")[: sums.size].reshape(sums.shape)
    means = totals / cell_count

    own_acc = solve_stream(warm_start, s_own, partner_pool, s_own * ORB, targets, tmat, y0)
    rem_acc = solve_stream(warm_start, s_rem, rem_block, zero, targets, tmat, y0)
    correction = mean_term(own_block, means[0]) + mean_term(rem_block, means[1])
    return (0.5 * coupling) * correction - (own_acc + rem_acc)


def solution(mesh):
    return jax.shard_map(
        body,
        mesh=mesh,
        in_specs=(
            P("band", "domain", None),
            P("band", "domain", None),
            P(),
            P(None, None, "band", "domain", None),
        ),
        out_specs=P("band", "domain", None),
        check_vma=False,
    )
```

```python
import functools
import math

import jax
import jax.numpy as jnp
from jax import lax
from jax.experimental import pallas as pl
from jax.experimental.pallas import tpu as pltpu
from jax.sharding import PartitionSpec as P

ORB = 8
STEPS = 2
SWEEPS = 3
GX = 192
GY = 192
GZ = 192


coupling = 4.0 * math.pi


def circulant(width):
    a = lax.broadcasted_iota(jnp.int32, (width, width), 0)
    b = lax.broadcasted_iota(jnp.int32, (width, width), 1)
    gap = (a - b + width) % width
    return ((gap == 1) | (gap == width - 1)).astype(jnp.bfloat16)


def stencil(y0, v, lo, hi, q, t_ref, wide):
    row_count = v.shape[0]
    halo = lo.shape[0]
    wide[0:halo, :] = lo
    wide[halo : halo + row_count, :] = v
    wide[halo + row_count : 2 * halo + row_count, :] = hi
    beside = wide[0:row_count, :] + wide[2 * halo : 2 * halo + row_count, :]
    down = wide[halo - 1 : halo - 1 + row_count, :]
    up = wide[halo + 1 : halo + 1 + row_count, :]
    down_wrap = wide[2 * halo - 1 : 2 * halo - 1 + row_count, :]
    up_wrap = wide[1 : 1 + row_count, :]
    y = lax.broadcasted_iota(jnp.int32, v.shape, 0) + y0
    for _ in range((row_count + GY - 2) // GY):
        y = jnp.where(y >= GY, y - GY, y)
    beside = beside + jnp.where(y == 0, down_wrap, down)
    beside = beside + jnp.where(y == GY - 1, up_wrap, up)
    high = v.astype(jnp.bfloat16)
    low = (v - high.astype(jnp.float32)).astype(jnp.bfloat16)
    tmat = t_ref[...]
    beside = beside + jnp.dot(high, tmat, preferred_element_type=jnp.float32)
    beside = beside + jnp.dot(low, tmat, preferred_element_type=jnp.float32)
    return (beside + coupling * q) * (1.0 / 6.0)


def sweep_kernel(final, sc_ref, v_ref, lo_ref, hi_ref, p_ref, t_ref, c_ref, *rest):
    y0 = sc_ref[0]
    part = p_ref[...].astype(jnp.float32)
    row_count = part.shape[0]
    halo = lo_ref.shape[-2]
    if final:
        acc_ref, wide = rest

        @pl.when(pl.program_id(0) == 0)
        def _():
            acc_ref[...] = jnp.zeros_like(acc_ref)

    else:
        out_ref, fwd_ref, bwd_ref, wide = rest
    for j in range(v_ref.shape[0]):
        q = part * t_ref[j]
        new = stencil(
            y0,
            v_ref[j].astype(jnp.float32),
            lo_ref[j].astype(jnp.float32),
            hi_ref[j].astype(jnp.float32),
            q,
            c_ref,
            wide,
        )
        if final:
            acc_ref[j] = acc_ref[j] + new * part
        else:
            out_ref[j] = new
            fwd_ref[j] = new[row_count - halo : row_count].astype(jnp.bfloat16)
            bwd_ref[j] = new[0:halo].astype(jnp.bfloat16)


def sweep_call(final, v, from_warm, lo, hi, partner, targets, tmat, scalars):
    orb, tgt, halo, width = lo.shape
    row_count = targets.shape[1]
    if from_warm:
        v_spec = pl.BlockSpec(
            (None, None, tgt, row_count, width), lambda i, sc: (sc[1], i, 0, 0, 0)
        )
    else:
        v_spec = pl.BlockSpec((None, tgt, row_count, width), lambda i, sc: (i, 0, 0, 0))
    h_spec = pl.BlockSpec((None, tgt, halo, width), lambda i, sc: (i, 0, 0, 0))
    p_spec = pl.BlockSpec((None, row_count, width), lambda i, sc: (sc[2] + i, 0, 0))
    t_spec = pl.BlockSpec((tgt, row_count, width), lambda i, sc: (0, 0, 0))
    c_spec = pl.BlockSpec((width, width), lambda i, sc: (0, 0))
    cells = orb * tgt * row_count * width
    if final:
        out_shape = jax.ShapeDtypeStruct((tgt, row_count, width), jnp.float32)
        out_specs = pl.BlockSpec((tgt, row_count, width), lambda i, sc: (0, 0, 0))
        out_bytes = tgt * row_count * width * 4
    else:
        out_shape = (
            jax.ShapeDtypeStruct((orb, tgt, row_count, width), jnp.float32),
            jax.ShapeDtypeStruct((orb, tgt, halo, width), jnp.bfloat16),
            jax.ShapeDtypeStruct((orb, tgt, halo, width), jnp.bfloat16),
        )
        out_specs = (
            pl.BlockSpec((None, tgt, row_count, width), lambda i, sc: (i, 0, 0, 0)),
            h_spec,
            h_spec,
        )
        out_bytes = cells * 4 + 2 * orb * tgt * halo * width * 2
    in_bytes = (
        cells * v.dtype.itemsize
        + 2 * orb * tgt * halo * width * 2
        + orb * row_count * width * 2
        + tgt * row_count * width * 4
    )
    grid_spec = pltpu.PrefetchScalarGridSpec(
        num_scalar_prefetch=1,
        grid=(orb,),
        in_specs=[v_spec, h_spec, h_spec, p_spec, t_spec, c_spec],
        out_specs=out_specs,
        scratch_shapes=[pltpu.VMEM((row_count + 2 * halo, width), jnp.float32)],
    )
    return pl.pallas_call(
        functools.partial(sweep_kernel, final),
        grid_spec=grid_spec,
        out_shape=out_shape,
        compiler_params=pltpu.CompilerParams(dimension_semantics=("arbitrary",)),
        cost_estimate=pl.CostEstimate(
            flops=cells * (4 * width + 24),
            transcendentals=0,
            bytes_accessed=in_bytes + out_bytes,
        ),
    )(scalars, v, lo, hi, partner, targets, tmat)


def exchange_halos(fwd, bwd):
    count = lax.axis_size("domain")
    forward = [(k, (k + 1) % count) for k in range(count)]
    backward = [((k + 1) % count, k) for k in range(count)]
    return lax.ppermute(fwd, "domain", forward), lax.ppermute(bwd, "domain", backward)


def solve_stream(warm_start, s, partner, pbase, targets, tmat, y0):
    row_count = targets.shape[1]
    halo = GY
    warm_block = lax.dynamic_index_in_dim(warm_start, s, 0, keepdims=False)
    lo, hi = exchange_halos(
        warm_block[:, :, row_count - halo :], warm_block[:, :, :halo]
    )
    scalars = jnp.stack([y0, s, pbase]).astype(jnp.int32)
    potential, fwd, bwd = sweep_call(
        False, warm_start, True, lo, hi, partner, targets, tmat, scalars
    )
    for sweep_index in range(1, SWEEPS - 1):
        lo, hi = exchange_halos(fwd, bwd)
        potential, fwd, bwd = sweep_call(
            False, potential, False, lo, hi, partner, targets, tmat, scalars
        )
    lo, hi = exchange_halos(fwd, bwd)
    return sweep_call(True, potential, False, lo, hi, partner, targets, tmat, scalars)


def butterfly_sum(x, axis):
    count = lax.axis_size(axis)
    step = 1
    while step < count:
        pairs = [(k, k ^ step) for k in range(count)]
        x = x + lax.ppermute(x, axis, pairs)
        step *= 2
    return x


def swap_over_y(block, mesh_shape):
    bands, domains = mesh_shape
    lanes = domains // 2
    def index(y, rest):
        return (y // 2) * domains + (y % 2) * lanes + rest
    ring = 2 * bands
    def shift(direction):
        return [
            (index(y, rest), index((y + direction) % ring, rest))
            for y in range(ring)
            for rest in range(lanes)
        ]
    half = block.shape[0] // 2
    axes = ("band", "domain")
    plus = lax.ppermute(lax.ppermute(block[:half], axes, shift(1)), axes, shift(1))
    minus = lax.ppermute(lax.ppermute(block[half:], axes, shift(-1)), axes, shift(-1))
    return jnp.concatenate([plus, minus], axis=0)


def pair_sums(block, targets):
    part = block.astype(jnp.float32)
    return jnp.sum(part[:, None] * targets[None], axis=(2, 3))


def mean_term(block, means):
    part = block.astype(jnp.float32)
    total = None
    for i in range(block.shape[0]):
        term = means[i][:, None, None] * part[i][None]
        total = term if total is None else total + term
    return total


def body(targets, partner_pool, owners, warm_start):
    row_count = targets.shape[1]
    cell_count = GX * GY * GZ
    domain = lax.axis_index("domain")
    band = lax.axis_index("band")
    y0 = (domain * row_count) % GY
    s_own = jnp.where(owners[0] == band, 0, 1).astype(jnp.int32)
    s_rem = 1 - s_own
    own_block = lax.dynamic_slice_in_dim(partner_pool, s_own * ORB, ORB, 0)
    rem_block = swap_over_y(own_block, (lax.axis_size("band"), lax.axis_size("domain")))
    tmat = circulant(targets.shape[2])
    zero = jnp.zeros((), jnp.int32)

    sums = jnp.stack([pair_sums(own_block, targets), pair_sums(rem_block, targets)])
    means = butterfly_sum(sums, "domain") / cell_count

    own_acc = solve_stream(warm_start, s_own, partner_pool, s_own * ORB, targets, tmat, y0)
    rem_acc = solve_stream(warm_start, s_rem, rem_block, zero, targets, tmat, y0)
    correction = mean_term(own_block, means[0]) + mean_term(rem_block, means[1])
    return (0.5 * coupling) * correction - (own_acc + rem_acc)


def solution(mesh):
    return jax.shard_map(
        body,
        mesh=mesh,
        in_specs=(
            P("band", "domain", None),
            P("band", "domain", None),
            P(),
            P(None, None, "band", "domain", None),
        ),
        out_specs=P("band", "domain", None),
        check_vma=False,
    )
```

```python
import functools
import math

import jax
import jax.numpy as jnp
from jax import lax
from jax.experimental import pallas as pl
from jax.experimental.pallas import tpu as pltpu
from jax.sharding import PartitionSpec as P

ORB = 8
STEPS = 2
SWEEPS = 3
GX = 192
GY = 192
GZ = 192


coupling = 4.0 * math.pi


def circulant(width):
    a = lax.broadcasted_iota(jnp.int32, (width, width), 0)
    b = lax.broadcasted_iota(jnp.int32, (width, width), 1)
    gap = (a - b + width) % width
    return ((gap == 1) | (gap == width - 1)).astype(jnp.bfloat16)


def stencil(y0, v, lo, hi, q, t_ref, wide):
    row_count = v.shape[0]
    halo = lo.shape[0]
    wide[0:halo, :] = lo
    wide[halo : halo + row_count, :] = v
    wide[halo + row_count : 2 * halo + row_count, :] = hi
    beside = wide[0:row_count, :] + wide[2 * halo : 2 * halo + row_count, :]
    down = wide[halo - 1 : halo - 1 + row_count, :]
    up = wide[halo + 1 : halo + 1 + row_count, :]
    down_wrap = wide[2 * halo - 1 : 2 * halo - 1 + row_count, :]
    up_wrap = wide[1 : 1 + row_count, :]
    y = lax.broadcasted_iota(jnp.int32, v.shape, 0) + y0
    for _ in range((row_count + GY - 2) // GY):
        y = jnp.where(y >= GY, y - GY, y)
    beside = beside + jnp.where(y == 0, down_wrap, down)
    beside = beside + jnp.where(y == GY - 1, up_wrap, up)
    high = v.astype(jnp.bfloat16)
    low = (v - high.astype(jnp.float32)).astype(jnp.bfloat16)
    tmat = t_ref[...]
    beside = beside + jnp.dot(high, tmat, preferred_element_type=jnp.float32)
    beside = beside + jnp.dot(low, tmat, preferred_element_type=jnp.float32)
    return (beside + coupling * q) * (1.0 / 6.0)


def sweep_kernel(final, sc_ref, v_ref, lo_ref, hi_ref, p_ref, t_ref, c_ref, *rest):
    y0 = sc_ref[0]
    part = p_ref[...].astype(jnp.float32)
    row_count = part.shape[0]
    halo = lo_ref.shape[-2]
    if final:
        acc_ref, wide = rest

        @pl.when(pl.program_id(0) == 0)
        def _():
            acc_ref[...] = jnp.zeros_like(acc_ref)

    else:
        out_ref, fwd_ref, bwd_ref, wide = rest
    for j in range(v_ref.shape[0]):
        q = part * t_ref[j]
        new = stencil(
            y0,
            v_ref[j].astype(jnp.float32),
            lo_ref[j].astype(jnp.float32),
            hi_ref[j].astype(jnp.float32),
            q,
            c_ref,
            wide,
        )
        if final:
            acc_ref[j] = acc_ref[j] + new * part
        else:
            out_ref[j] = new
            fwd_ref[j] = new[row_count - halo : row_count].astype(jnp.bfloat16)
            bwd_ref[j] = new[0:halo].astype(jnp.bfloat16)


def sweep_call(final, v, from_warm, lo, hi, partner, targets, tmat, scalars):
    orb, tgt, halo, width = lo.shape
    row_count = targets.shape[1]
    if from_warm:
        v_spec = pl.BlockSpec(
            (None, None, tgt, row_count, width), lambda i, sc: (sc[1], i, 0, 0, 0)
        )
    else:
        v_spec = pl.BlockSpec((None, tgt, row_count, width), lambda i, sc: (i, 0, 0, 0))
    h_spec = pl.BlockSpec((None, tgt, halo, width), lambda i, sc: (i, 0, 0, 0))
    p_spec = pl.BlockSpec((None, row_count, width), lambda i, sc: (sc[2] + i, 0, 0))
    t_spec = pl.BlockSpec((tgt, row_count, width), lambda i, sc: (0, 0, 0))
    c_spec = pl.BlockSpec((width, width), lambda i, sc: (0, 0))
    cells = orb * tgt * row_count * width
    if final:
        out_shape = jax.ShapeDtypeStruct((tgt, row_count, width), jnp.float32)
        out_specs = pl.BlockSpec((tgt, row_count, width), lambda i, sc: (0, 0, 0))
        out_bytes = tgt * row_count * width * 4
    else:
        out_shape = (
            jax.ShapeDtypeStruct((orb, tgt, row_count, width), jnp.float32),
            jax.ShapeDtypeStruct((orb, tgt, halo, width), jnp.bfloat16),
            jax.ShapeDtypeStruct((orb, tgt, halo, width), jnp.bfloat16),
        )
        out_specs = (
            pl.BlockSpec((None, tgt, row_count, width), lambda i, sc: (i, 0, 0, 0)),
            h_spec,
            h_spec,
        )
        out_bytes = cells * 4 + 2 * orb * tgt * halo * width * 2
    in_bytes = (
        cells * v.dtype.itemsize
        + 2 * orb * tgt * halo * width * 2
        + orb * row_count * width * 2
        + tgt * row_count * width * 4
    )
    grid_spec = pltpu.PrefetchScalarGridSpec(
        num_scalar_prefetch=1,
        grid=(orb,),
        in_specs=[v_spec, h_spec, h_spec, p_spec, t_spec, c_spec],
        out_specs=out_specs,
        scratch_shapes=[pltpu.VMEM((row_count + 2 * halo, width), jnp.float32)],
    )
    return pl.pallas_call(
        functools.partial(sweep_kernel, final),
        grid_spec=grid_spec,
        out_shape=out_shape,
        compiler_params=pltpu.CompilerParams(dimension_semantics=("arbitrary",)),
        cost_estimate=pl.CostEstimate(
            flops=cells * (4 * width + 24),
            transcendentals=0,
            bytes_accessed=in_bytes + out_bytes,
        ),
    )(scalars, v, lo, hi, partner, targets, tmat)


def exchange_halos(fwd, bwd):
    count = lax.axis_size("domain")
    forward = [(k, (k + 1) % count) for k in range(count)]
    backward = [((k + 1) % count, k) for k in range(count)]
    return lax.ppermute(fwd, "domain", forward), lax.ppermute(bwd, "domain", backward)


def warm_halos(warm_start, s, row_count):
    warm_block = lax.dynamic_index_in_dim(warm_start, s, 0, keepdims=False)
    return warm_block[:, :, row_count - GY :], warm_block[:, :, :GY]


def finish_stream(potential, fwd, bwd, partner, targets, tmat, scalars):
    for sweep_index in range(1, SWEEPS - 1):
        lo, hi = exchange_halos(fwd, bwd)
        potential, fwd, bwd = sweep_call(
            False, potential, False, lo, hi, partner, targets, tmat, scalars
        )
    lo, hi = exchange_halos(fwd, bwd)
    return sweep_call(True, potential, False, lo, hi, partner, targets, tmat, scalars)


def butterfly_sum(x, axis):
    count = lax.axis_size(axis)
    step = 1
    while step < count:
        radix = 2
        total = x
        for part in range(1, radix):
            pairs = [
                (k, (k // (step * radix)) * step * radix + ((k // step) % radix ^ part) * step + k % step)
                for k in range(count)
            ]
            total = total + lax.ppermute(x, axis, pairs)
        x = total
        step *= radix
    return x


def swap_over_y(block, mesh_shape):
    bands, domains = mesh_shape
    lanes = domains // 2
    def index(y, rest):
        return (y // 2) * domains + (y % 2) * lanes + rest
    ring = 2 * bands
    def shift(direction):
        return [
            (index(y, rest), index((y + direction) % ring, rest))
            for y in range(ring)
            for rest in range(lanes)
        ]
    half = block.shape[0] // 2
    axes = ("band", "domain")
    plus = lax.ppermute(block[:half], axes, shift(1))
    minus = lax.ppermute(block[half:], axes, shift(-1))
    return plus, minus, lambda plus, minus: jnp.concatenate(
        [lax.ppermute(plus, axes, shift(1)), lax.ppermute(minus, axes, shift(-1))], axis=0
    )


def pair_sums(block, targets):
    part = block.astype(jnp.float32)
    return jnp.sum(part[:, None] * targets[None], axis=(2, 3))


def mean_term(block, means):
    part = block.astype(jnp.float32)
    total = None
    for i in range(block.shape[0]):
        term = means[i][:, None, None] * part[i][None]
        total = term if total is None else total + term
    return total


def body(targets, partner_pool, owners, warm_start):
    row_count = targets.shape[1]
    cell_count = GX * GY * GZ
    domain = lax.axis_index("domain")
    band = lax.axis_index("band")
    y0 = (domain * row_count) % GY
    s_own = jnp.where(owners[0] == band, 0, 1).astype(jnp.int32)
    s_rem = 1 - s_own
    own_block = lax.dynamic_slice_in_dim(partner_pool, s_own * ORB, ORB, 0)
    tmat = circulant(targets.shape[2])
    own_scalars = jnp.stack([y0, s_own, s_own * ORB]).astype(jnp.int32)
    rem_scalars = jnp.stack([y0, s_rem, jnp.zeros((), jnp.int32)]).astype(jnp.int32)

    own_halos = exchange_halos(*warm_halos(warm_start, s_own, row_count))
    rem_sends, own_halos = lax.optimization_barrier(
        (warm_halos(warm_start, s_rem, row_count), own_halos)
    )
    rem_halos = exchange_halos(*rem_sends)
    plus, minus, finish_swap = swap_over_y(
        own_block, (lax.axis_size("band"), lax.axis_size("domain"))
    )
    potential, fwd, bwd = sweep_call(
        False, warm_start, True, *own_halos, partner_pool, targets, tmat, own_scalars
    )
    (plus, minus), potential = lax.optimization_barrier(((plus, minus), potential))
    rem_block = finish_swap(plus, minus)
    rem_state = sweep_call(
        False, warm_start, True, *rem_halos, rem_block, targets, tmat, rem_scalars
    )

    sums = jnp.stack([pair_sums(own_block, targets), pair_sums(rem_block, targets)])
    means = butterfly_sum(sums, "domain") / cell_count

    own_acc = finish_stream(potential, fwd, bwd, partner_pool, targets, tmat, own_scalars)
    rem_acc = finish_stream(*rem_state, rem_block, targets, tmat, rem_scalars)
    correction = mean_term(own_block, means[0]) + mean_term(rem_block, means[1])
    return (0.5 * coupling) * correction - (own_acc + rem_acc)


def solution(mesh):
    return jax.shard_map(
        body,
        mesh=mesh,
        in_specs=(
            P("band", "domain", None),
            P("band", "domain", None),
            P(),
            P(None, None, "band", "domain", None),
        ),
        out_specs=P("band", "domain", None),
        check_vma=False,
    )
```

```python
import functools
import math

import jax
import jax.numpy as jnp
from jax import lax
from jax.experimental import pallas as pl
from jax.experimental.pallas import tpu as pltpu
from jax.sharding import PartitionSpec as P

ORB = 8
STEPS = 2
SWEEPS = 3
GX = 192
GY = 192
GZ = 192


coupling = 4.0 * math.pi


def circulant(width):
    a = lax.broadcasted_iota(jnp.int32, (width, width), 0)
    b = lax.broadcasted_iota(jnp.int32, (width, width), 1)
    gap = (a - b + width) % width
    return ((gap == 1) | (gap == width - 1)).astype(jnp.bfloat16)


def stencil(y0, v, lo, hi, q, t_ref, wide):
    row_count = v.shape[0]
    halo = lo.shape[0]
    wide[0:halo, :] = lo
    wide[halo : halo + row_count, :] = v
    wide[halo + row_count : 2 * halo + row_count, :] = hi
    beside = wide[0:row_count, :] + wide[2 * halo : 2 * halo + row_count, :]
    down = wide[halo - 1 : halo - 1 + row_count, :]
    up = wide[halo + 1 : halo + 1 + row_count, :]
    down_wrap = wide[2 * halo - 1 : 2 * halo - 1 + row_count, :]
    up_wrap = wide[1 : 1 + row_count, :]
    y = lax.broadcasted_iota(jnp.int32, v.shape, 0) + y0
    for _ in range((row_count + GY - 2) // GY):
        y = jnp.where(y >= GY, y - GY, y)
    beside = beside + jnp.where(y == 0, down_wrap, down)
    beside = beside + jnp.where(y == GY - 1, up_wrap, up)
    high = v.astype(jnp.bfloat16)
    low = (v - high.astype(jnp.float32)).astype(jnp.bfloat16)
    tmat = t_ref[...]
    beside = beside + jnp.dot(high, tmat, preferred_element_type=jnp.float32)
    beside = beside + jnp.dot(low, tmat, preferred_element_type=jnp.float32)
    return (beside + coupling * q) * (1.0 / 6.0)


def sweep_kernel(final, sc_ref, v_ref, lo_ref, hi_ref, p_ref, t_ref, c_ref, *rest):
    y0 = sc_ref[0]
    part = p_ref[...].astype(jnp.float32)
    row_count = part.shape[0]
    halo = lo_ref.shape[-2]
    if final:
        acc_ref, wide = rest

        @pl.when(pl.program_id(0) == 0)
        def _():
            acc_ref[...] = jnp.zeros_like(acc_ref)

    else:
        out_ref, fwd_ref, bwd_ref, wide = rest
    for j in range(v_ref.shape[0]):
        q = part * t_ref[j]
        new = stencil(
            y0,
            v_ref[j].astype(jnp.float32),
            lo_ref[j].astype(jnp.float32),
            hi_ref[j].astype(jnp.float32),
            q,
            c_ref,
            wide,
        )
        if final:
            acc_ref[j] = acc_ref[j] + new * part
        else:
            out_ref[j] = new
            fwd_ref[j] = new[row_count - halo : row_count].astype(jnp.bfloat16)
            bwd_ref[j] = new[0:halo].astype(jnp.bfloat16)


def sweep_call(final, v, from_warm, lo, hi, partner, targets, tmat, scalars):
    orb, tgt, halo, width = lo.shape
    row_count = targets.shape[1]
    if from_warm:
        v_spec = pl.BlockSpec(
            (None, None, tgt, row_count, width), lambda i, sc: (sc[1], i, 0, 0, 0)
        )
    else:
        v_spec = pl.BlockSpec((None, tgt, row_count, width), lambda i, sc: (i, 0, 0, 0))
    h_spec = pl.BlockSpec((None, tgt, halo, width), lambda i, sc: (i, 0, 0, 0))
    p_spec = pl.BlockSpec((None, row_count, width), lambda i, sc: (sc[2] + i, 0, 0))
    t_spec = pl.BlockSpec((tgt, row_count, width), lambda i, sc: (0, 0, 0))
    c_spec = pl.BlockSpec((width, width), lambda i, sc: (0, 0))
    cells = orb * tgt * row_count * width
    if final:
        out_shape = jax.ShapeDtypeStruct((tgt, row_count, width), jnp.float32)
        out_specs = pl.BlockSpec((tgt, row_count, width), lambda i, sc: (0, 0, 0))
        out_bytes = tgt * row_count * width * 4
    else:
        out_shape = (
            jax.ShapeDtypeStruct((orb, tgt, row_count, width), jnp.float32),
            jax.ShapeDtypeStruct((orb, tgt, halo, width), jnp.bfloat16),
            jax.ShapeDtypeStruct((orb, tgt, halo, width), jnp.bfloat16),
        )
        out_specs = (
            pl.BlockSpec((None, tgt, row_count, width), lambda i, sc: (i, 0, 0, 0)),
            h_spec,
            h_spec,
        )
        out_bytes = cells * 4 + 2 * orb * tgt * halo * width * 2
    in_bytes = (
        cells * v.dtype.itemsize
        + 2 * orb * tgt * halo * width * 2
        + orb * row_count * width * 2
        + tgt * row_count * width * 4
    )
    grid_spec = pltpu.PrefetchScalarGridSpec(
        num_scalar_prefetch=1,
        grid=(orb,),
        in_specs=[v_spec, h_spec, h_spec, p_spec, t_spec, c_spec],
        out_specs=out_specs,
        scratch_shapes=[pltpu.VMEM((row_count + 2 * halo, width), jnp.float32)],
    )
    return pl.pallas_call(
        functools.partial(sweep_kernel, final),
        grid_spec=grid_spec,
        out_shape=out_shape,
        compiler_params=pltpu.CompilerParams(dimension_semantics=("arbitrary",)),
        cost_estimate=pl.CostEstimate(
            flops=cells * (4 * width + 24),
            transcendentals=0,
            bytes_accessed=in_bytes + out_bytes,
        ),
    )(scalars, v, lo, hi, partner, targets, tmat)


def exchange_halos(fwd, bwd):
    count = lax.axis_size("domain")
    forward = [(k, (k + 1) % count) for k in range(count)]
    backward = [((k + 1) % count, k) for k in range(count)]
    return lax.ppermute(fwd, "domain", forward), lax.ppermute(bwd, "domain", backward)


def warm_halos(warm_start, s, row_count):
    warm_block = lax.dynamic_index_in_dim(warm_start, s, 0, keepdims=False)
    return warm_block[:, :, row_count - GY :], warm_block[:, :, :GY]


def finish_stream(potential, fwd, bwd, partner, targets, tmat, scalars):
    for sweep_index in range(1, SWEEPS - 1):
        lo, hi = exchange_halos(fwd, bwd)
        potential, fwd, bwd = sweep_call(
            False, potential, False, lo, hi, partner, targets, tmat, scalars
        )
    lo, hi = exchange_halos(fwd, bwd)
    return sweep_call(True, potential, False, lo, hi, partner, targets, tmat, scalars)


def butterfly_sum(x, axis):
    count = lax.axis_size(axis)
    step = 1
    while step < count:
        radix = 2
        total = x
        for part in range(1, radix):
            pairs = [
                (k, (k // (step * radix)) * step * radix + ((k // step) % radix ^ part) * step + k % step)
                for k in range(count)
            ]
            total = total + lax.ppermute(x, axis, pairs)
        x = total
        step *= radix
    return x


def swap_over_y(block, mesh_shape):
    bands, domains = mesh_shape
    lanes = domains // 2
    def index(y, rest):
        return (y // 2) * domains + (y % 2) * lanes + rest
    ring = 2 * bands
    def shift(direction):
        return [
            (index(y, rest), index((y + direction) % ring, rest))
            for y in range(ring)
            for rest in range(lanes)
        ]
    half = block.shape[0] // 2
    axes = ("band", "domain")
    plus = lax.ppermute(block[:half], axes, shift(1))
    minus = lax.ppermute(block[half:], axes, shift(-1))
    return plus, minus, lambda plus, minus: jnp.concatenate(
        [lax.ppermute(plus, axes, shift(1)), lax.ppermute(minus, axes, shift(-1))], axis=0
    )


def pair_sums(block, targets):
    part = block.astype(jnp.float32)
    return jnp.sum(part[:, None] * targets[None], axis=(2, 3))


def mean_term(block, means):
    part = block.astype(jnp.float32)
    total = None
    for i in range(block.shape[0]):
        term = means[i][:, None, None] * part[i][None]
        total = term if total is None else total + term
    return total


def body(targets, partner_pool, owners, warm_start):
    row_count = targets.shape[1]
    cell_count = GX * GY * GZ
    domain = lax.axis_index("domain")
    band = lax.axis_index("band")
    y0 = (domain * row_count) % GY
    s_own = jnp.where(owners[0] == band, 0, 1).astype(jnp.int32)
    s_rem = 1 - s_own
    own_block = lax.dynamic_slice_in_dim(partner_pool, s_own * ORB, ORB, 0)
    tmat = circulant(targets.shape[2])
    own_scalars = jnp.stack([y0, s_own, s_own * ORB]).astype(jnp.int32)
    rem_scalars = jnp.stack([y0, s_rem, jnp.zeros((), jnp.int32)]).astype(jnp.int32)

    own_halos = exchange_halos(*warm_halos(warm_start, s_own, row_count))
    plus, minus, finish_swap = swap_over_y(
        own_block, (lax.axis_size("band"), lax.axis_size("domain"))
    )
    rem_sends, own_halos, plus, minus = lax.optimization_barrier(
        (warm_halos(warm_start, s_rem, row_count), own_halos, plus, minus)
    )
    rem_halos = exchange_halos(*rem_sends)
    rem_block = finish_swap(plus, minus)
    potential, fwd, bwd = sweep_call(
        False, warm_start, True, *own_halos, partner_pool, targets, tmat, own_scalars
    )
    rem_state = sweep_call(
        False, warm_start, True, *rem_halos, rem_block, targets, tmat, rem_scalars
    )

    sums = jnp.stack([pair_sums(own_block, targets), pair_sums(rem_block, targets)])
    means = butterfly_sum(sums, "domain") / cell_count

    own_acc = finish_stream(potential, fwd, bwd, partner_pool, targets, tmat, own_scalars)
    rem_acc = finish_stream(*rem_state, rem_block, targets, tmat, rem_scalars)
    correction = mean_term(own_block, means[0]) + mean_term(rem_block, means[1])
    return (0.5 * coupling) * correction - (own_acc + rem_acc)


def solution(mesh):
    return jax.shard_map(
        body,
        mesh=mesh,
        in_specs=(
            P("band", "domain", None),
            P("band", "domain", None),
            P(),
            P(None, None, "band", "domain", None),
        ),
        out_specs=P("band", "domain", None),
        check_vma=False,
    )
```

```python
import functools
import math

import jax
import jax.numpy as jnp
from jax import lax
from jax.experimental import pallas as pl
from jax.experimental.pallas import tpu as pltpu
from jax.sharding import PartitionSpec as P

ORB = 8
STEPS = 2
SWEEPS = 3
GX = 192
GY = 192
GZ = 192


coupling = 4.0 * math.pi


def circulant(width):
    a = lax.broadcasted_iota(jnp.int32, (width, width), 0)
    b = lax.broadcasted_iota(jnp.int32, (width, width), 1)
    gap = (a - b + width) % width
    return ((gap == 1) | (gap == width - 1)).astype(jnp.bfloat16)


def split_dot(lhs, rhs, left):
    high = lhs.astype(jnp.bfloat16)
    low = (lhs - high.astype(jnp.float32)).astype(jnp.bfloat16)
    if left:
        return jnp.dot(rhs, high, preferred_element_type=jnp.float32) + jnp.dot(
            rhs, low, preferred_element_type=jnp.float32
        )
    return jnp.dot(high, rhs, preferred_element_type=jnp.float32) + jnp.dot(
        low, rhs, preferred_element_type=jnp.float32
    )


def stencil(y0, v, lo, hi, q, ty_ref, tz_ref, wide, inner):
    row_count = v.shape[0]
    halo = lo.shape[0]
    wide[0:halo, :] = lo
    wide[halo : halo + row_count, :] = v
    wide[halo + row_count : 2 * halo + row_count, :] = hi
    ty = ty_ref[...]
    tz = tz_ref[...]
    first = pl.multiple_of(GY - y0, 8)
    for plane in range(inner.shape[0] // GY):
        block = wide[pl.ds(first + plane * GY, GY), :]
        inner[plane * GY : (plane + 1) * GY, :] = split_dot(block, ty, True) + split_dot(
            block, tz, False
        )
    beside = wide[0:row_count, :] + wide[2 * halo : 2 * halo + row_count, :]
    beside = beside + inner[pl.ds(pl.multiple_of(y0, 8), row_count), :]
    return (beside + coupling * q) * (1.0 / 6.0)


def sweep_kernel(final, sc_ref, v_ref, lo_ref, hi_ref, p_ref, t_ref, cy_ref, cz_ref, *rest):
    y0 = sc_ref[0]
    part = p_ref[...].astype(jnp.float32)
    row_count = part.shape[0]
    halo = lo_ref.shape[-2]
    if final:
        acc_ref, wide, inner = rest

        @pl.when(pl.program_id(0) == 0)
        def _():
            acc_ref[...] = jnp.zeros_like(acc_ref)

    else:
        out_ref, fwd_ref, bwd_ref, wide, inner = rest
    for j in range(v_ref.shape[0]):
        q = part * t_ref[j]
        new = stencil(
            y0,
            v_ref[j].astype(jnp.float32),
            lo_ref[j].astype(jnp.float32),
            hi_ref[j].astype(jnp.float32),
            q,
            cy_ref,
            cz_ref,
            wide,
            inner,
        )
        if final:
            acc_ref[j] = acc_ref[j] + new * part
        else:
            out_ref[j] = new
            fwd_ref[j] = new[row_count - halo : row_count].astype(jnp.bfloat16)
            bwd_ref[j] = new[0:halo].astype(jnp.bfloat16)


def sweep_call(final, v, from_warm, lo, hi, partner, targets, tmats, scalars):
    orb, tgt, halo, width = lo.shape
    row_count = targets.shape[1]
    if from_warm:
        v_spec = pl.BlockSpec(
            (None, None, tgt, row_count, width), lambda i, sc: (sc[1], i, 0, 0, 0)
        )
    else:
        v_spec = pl.BlockSpec((None, tgt, row_count, width), lambda i, sc: (i, 0, 0, 0))
    h_spec = pl.BlockSpec((None, tgt, halo, width), lambda i, sc: (i, 0, 0, 0))
    p_spec = pl.BlockSpec((None, row_count, width), lambda i, sc: (sc[2] + i, 0, 0))
    t_spec = pl.BlockSpec((tgt, row_count, width), lambda i, sc: (0, 0, 0))
    cy_spec = pl.BlockSpec((GY, GY), lambda i, sc: (0, 0))
    cz_spec = pl.BlockSpec((width, width), lambda i, sc: (0, 0))
    planes = -(-(row_count + GY - math.gcd(row_count, GY)) // GY)
    cells = orb * tgt * row_count * width
    if final:
        out_shape = jax.ShapeDtypeStruct((tgt, row_count, width), jnp.float32)
        out_specs = pl.BlockSpec((tgt, row_count, width), lambda i, sc: (0, 0, 0))
        out_bytes = tgt * row_count * width * 4
    else:
        out_shape = (
            jax.ShapeDtypeStruct((orb, tgt, row_count, width), jnp.float32),
            jax.ShapeDtypeStruct((orb, tgt, halo, width), jnp.bfloat16),
            jax.ShapeDtypeStruct((orb, tgt, halo, width), jnp.bfloat16),
        )
        out_specs = (
            pl.BlockSpec((None, tgt, row_count, width), lambda i, sc: (i, 0, 0, 0)),
            h_spec,
            h_spec,
        )
        out_bytes = cells * 4 + 2 * orb * tgt * halo * width * 2
    in_bytes = (
        cells * v.dtype.itemsize
        + 2 * orb * tgt * halo * width * 2
        + orb * row_count * width * 2
        + tgt * row_count * width * 4
    )
    grid_spec = pltpu.PrefetchScalarGridSpec(
        num_scalar_prefetch=1,
        grid=(orb,),
        in_specs=[v_spec, h_spec, h_spec, p_spec, t_spec, cy_spec, cz_spec],
        out_specs=out_specs,
        scratch_shapes=[
            pltpu.VMEM((row_count + 2 * halo, width), jnp.float32),
            pltpu.VMEM((planes * GY, width), jnp.float32),
        ],
    )
    return pl.pallas_call(
        functools.partial(sweep_kernel, final),
        grid_spec=grid_spec,
        out_shape=out_shape,
        compiler_params=pltpu.CompilerParams(dimension_semantics=("arbitrary",)),
        cost_estimate=pl.CostEstimate(
            flops=cells * (8 * width + 16),
            transcendentals=0,
            bytes_accessed=in_bytes + out_bytes,
        ),
    )(scalars, v, lo, hi, partner, targets, *tmats)


def exchange_halos(fwd, bwd):
    count = lax.axis_size("domain")
    forward = [(k, (k + 1) % count) for k in range(count)]
    backward = [((k + 1) % count, k) for k in range(count)]
    return lax.ppermute(fwd, "domain", forward), lax.ppermute(bwd, "domain", backward)


def warm_halos(warm_start, s, row_count):
    warm_block = lax.dynamic_index_in_dim(warm_start, s, 0, keepdims=False)
    return warm_block[:, :, row_count - GY :], warm_block[:, :, :GY]


def finish_stream(potential, fwd, bwd, partner, targets, tmat, scalars):
    for sweep_index in range(1, SWEEPS - 1):
        lo, hi = exchange_halos(fwd, bwd)
        potential, fwd, bwd = sweep_call(
            False, potential, False, lo, hi, partner, targets, tmat, scalars
        )
    lo, hi = exchange_halos(fwd, bwd)
    return sweep_call(True, potential, False, lo, hi, partner, targets, tmat, scalars)


def butterfly_sum(x, axis):
    count = lax.axis_size(axis)
    step = 1
    while step < count:
        radix = 2
        total = x
        for part in range(1, radix):
            pairs = [
                (k, (k // (step * radix)) * step * radix + ((k // step) % radix ^ part) * step + k % step)
                for k in range(count)
            ]
            total = total + lax.ppermute(x, axis, pairs)
        x = total
        step *= radix
    return x


def swap_over_y(block, mesh_shape):
    bands, domains = mesh_shape
    lanes = domains // 2
    def index(y, rest):
        return (y // 2) * domains + (y % 2) * lanes + rest
    ring = 2 * bands
    def shift(direction):
        return [
            (index(y, rest), index((y + direction) % ring, rest))
            for y in range(ring)
            for rest in range(lanes)
        ]
    half = block.shape[0] // 2
    axes = ("band", "domain")
    plus = lax.ppermute(block[:half], axes, shift(1))
    minus = lax.ppermute(block[half:], axes, shift(-1))
    return plus, minus, lambda plus, minus: jnp.concatenate(
        [lax.ppermute(plus, axes, shift(1)), lax.ppermute(minus, axes, shift(-1))], axis=0
    )


def pair_sums(block, targets):
    part = block.astype(jnp.float32)
    return jnp.sum(part[:, None] * targets[None], axis=(2, 3))


def mean_term(block, means):
    part = block.astype(jnp.float32)
    total = None
    for i in range(block.shape[0]):
        term = means[i][:, None, None] * part[i][None]
        total = term if total is None else total + term
    return total


def body(targets, partner_pool, owners, warm_start):
    row_count = targets.shape[1]
    cell_count = GX * GY * GZ
    domain = lax.axis_index("domain")
    band = lax.axis_index("band")
    y0 = (domain * row_count) % GY
    s_own = jnp.where(owners[0] == band, 0, 1).astype(jnp.int32)
    s_rem = 1 - s_own
    own_block = lax.dynamic_slice_in_dim(partner_pool, s_own * ORB, ORB, 0)
    tmat = (circulant(GY), circulant(targets.shape[2]))
    own_scalars = jnp.stack([y0, s_own, s_own * ORB]).astype(jnp.int32)
    rem_scalars = jnp.stack([y0, s_rem, jnp.zeros((), jnp.int32)]).astype(jnp.int32)

    own_halos = exchange_halos(*warm_halos(warm_start, s_own, row_count))
    plus, minus, finish_swap = swap_over_y(
        own_block, (lax.axis_size("band"), lax.axis_size("domain"))
    )
    rem_sends, own_halos, plus, minus = lax.optimization_barrier(
        (warm_halos(warm_start, s_rem, row_count), own_halos, plus, minus)
    )
    rem_halos = exchange_halos(*rem_sends)
    rem_block = finish_swap(plus, minus)
    potential, fwd, bwd = sweep_call(
        False, warm_start, True, *own_halos, partner_pool, targets, tmat, own_scalars
    )
    rem_state = sweep_call(
        False, warm_start, True, *rem_halos, rem_block, targets, tmat, rem_scalars
    )

    sums = jnp.stack([pair_sums(own_block, targets), pair_sums(rem_block, targets)])
    means = butterfly_sum(sums, "domain") / cell_count

    own_acc = finish_stream(potential, fwd, bwd, partner_pool, targets, tmat, own_scalars)
    rem_acc = finish_stream(*rem_state, rem_block, targets, tmat, rem_scalars)
    correction = mean_term(own_block, means[0]) + mean_term(rem_block, means[1])
    return (0.5 * coupling) * correction - (own_acc + rem_acc)


def solution(mesh):
    return jax.shard_map(
        body,
        mesh=mesh,
        in_specs=(
            P("band", "domain", None),
            P("band", "domain", None),
            P(),
            P(None, None, "band", "domain", None),
        ),
        out_specs=P("band", "domain", None),
        check_vma=False,
    )
```

```python
import functools
import math

import jax
import jax.numpy as jnp
from jax import lax
from jax.experimental import pallas as pl
from jax.experimental.pallas import tpu as pltpu
from jax.sharding import PartitionSpec as P

ORB = 8
STEPS = 2
SWEEPS = 3
GX = 192
GY = 192
GZ = 192


coupling = 4.0 * math.pi


def circulant(width):
    a = lax.broadcasted_iota(jnp.int32, (width, width), 0)
    b = lax.broadcasted_iota(jnp.int32, (width, width), 1)
    gap = (a - b + width) % width
    return ((gap == 1) | (gap == width - 1)).astype(jnp.bfloat16)


def split_dot(lhs, rhs, left):
    high = lhs.astype(jnp.bfloat16)
    low = (lhs - high.astype(jnp.float32)).astype(jnp.bfloat16)
    if left:
        return jnp.dot(rhs, high, preferred_element_type=jnp.float32) + jnp.dot(
            rhs, low, preferred_element_type=jnp.float32
        )
    return jnp.dot(high, rhs, preferred_element_type=jnp.float32) + jnp.dot(
        low, rhs, preferred_element_type=jnp.float32
    )


def stencil(y0, v, lo, hi, q, ty_ref, tz_ref, wide, inner):
    row_count = v.shape[0]
    halo = lo.shape[0]
    wide[0:halo, :] = lo
    wide[halo : halo + row_count, :] = v
    wide[halo + row_count : 2 * halo + row_count, :] = hi
    ty = ty_ref[...]
    tz = tz_ref[...]
    first = pl.multiple_of(GY - y0, 8)
    for plane in range(inner.shape[0] // GY):
        block = wide[pl.ds(first + plane * GY, GY), :]
        inner[plane * GY : (plane + 1) * GY, :] = split_dot(block, ty, True) + split_dot(
            block, tz, False
        )
    beside = wide[0:row_count, :] + wide[2 * halo : 2 * halo + row_count, :]
    beside = beside + inner[pl.ds(pl.multiple_of(y0, 8), row_count), :]
    return (beside + coupling * q) * (1.0 / 6.0)


def sweep_kernel(final, sc_ref, v_ref, lo_ref, hi_ref, p_ref, t_ref, cy_ref, cz_ref, *rest):
    y0 = sc_ref[0]
    part = p_ref[...].astype(jnp.float32)
    row_count = part.shape[0]
    halo = lo_ref.shape[-2]
    if final:
        acc_ref, wide, inner = rest

        @pl.when(pl.program_id(0) == 0)
        def _():
            acc_ref[...] = jnp.zeros_like(acc_ref)

    else:
        out_ref, fwd_ref, bwd_ref, wide, inner = rest
    for j in range(v_ref.shape[0]):
        q = part * t_ref[j]
        new = stencil(
            y0,
            v_ref[j].astype(jnp.float32),
            lo_ref[j].astype(jnp.float32),
            hi_ref[j].astype(jnp.float32),
            q,
            cy_ref,
            cz_ref,
            wide,
            inner,
        )
        if final:
            acc_ref[j] = acc_ref[j] + new * part
        else:
            rounded = new.astype(jnp.bfloat16)
            out_ref[j] = rounded
            fwd_ref[j] = rounded[row_count - halo : row_count]
            bwd_ref[j] = rounded[0:halo]


def sweep_call(final, v, from_warm, lo, hi, partner, targets, tmats, scalars):
    orb, tgt, halo, width = lo.shape
    row_count = targets.shape[1]
    if from_warm:
        v_spec = pl.BlockSpec(
            (None, None, tgt, row_count, width), lambda i, sc: (sc[1], i, 0, 0, 0)
        )
    else:
        v_spec = pl.BlockSpec((None, tgt, row_count, width), lambda i, sc: (i, 0, 0, 0))
    h_spec = pl.BlockSpec((None, tgt, halo, width), lambda i, sc: (i, 0, 0, 0))
    p_spec = pl.BlockSpec((None, row_count, width), lambda i, sc: (sc[2] + i, 0, 0))
    t_spec = pl.BlockSpec((tgt, row_count, width), lambda i, sc: (0, 0, 0))
    cy_spec = pl.BlockSpec((GY, GY), lambda i, sc: (0, 0))
    cz_spec = pl.BlockSpec((width, width), lambda i, sc: (0, 0))
    planes = -(-(row_count + GY - math.gcd(row_count, GY)) // GY)
    cells = orb * tgt * row_count * width
    if final:
        out_shape = jax.ShapeDtypeStruct((tgt, row_count, width), jnp.float32)
        out_specs = pl.BlockSpec((tgt, row_count, width), lambda i, sc: (0, 0, 0))
        out_bytes = tgt * row_count * width * 4
    else:
        out_shape = (
            jax.ShapeDtypeStruct((orb, tgt, row_count, width), jnp.bfloat16),
            jax.ShapeDtypeStruct((orb, tgt, halo, width), jnp.bfloat16),
            jax.ShapeDtypeStruct((orb, tgt, halo, width), jnp.bfloat16),
        )
        out_specs = (
            pl.BlockSpec((None, tgt, row_count, width), lambda i, sc: (i, 0, 0, 0)),
            h_spec,
            h_spec,
        )
        out_bytes = cells * 2 + 2 * orb * tgt * halo * width * 2
    in_bytes = (
        cells * v.dtype.itemsize
        + 2 * orb * tgt * halo * width * 2
        + orb * row_count * width * 2
        + tgt * row_count * width * 4
    )
    grid_spec = pltpu.PrefetchScalarGridSpec(
        num_scalar_prefetch=1,
        grid=(orb,),
        in_specs=[v_spec, h_spec, h_spec, p_spec, t_spec, cy_spec, cz_spec],
        out_specs=out_specs,
        scratch_shapes=[
            pltpu.VMEM((row_count + 2 * halo, width), jnp.float32),
            pltpu.VMEM((planes * GY, width), jnp.float32),
        ],
    )
    return pl.pallas_call(
        functools.partial(sweep_kernel, final),
        grid_spec=grid_spec,
        out_shape=out_shape,
        compiler_params=pltpu.CompilerParams(dimension_semantics=("arbitrary",)),
        cost_estimate=pl.CostEstimate(
            flops=cells * (8 * width + 16),
            transcendentals=0,
            bytes_accessed=in_bytes + out_bytes,
        ),
    )(scalars, v, lo, hi, partner, targets, *tmats)


def exchange_halos(fwd, bwd):
    count = lax.axis_size("domain")
    forward = [(k, (k + 1) % count) for k in range(count)]
    backward = [((k + 1) % count, k) for k in range(count)]
    return lax.ppermute(fwd, "domain", forward), lax.ppermute(bwd, "domain", backward)


def warm_halos(warm_start, s, row_count):
    warm_block = lax.dynamic_index_in_dim(warm_start, s, 0, keepdims=False)
    return warm_block[:, :, row_count - GY :], warm_block[:, :, :GY]


def finish_stream(potential, fwd, bwd, partner, targets, tmat, scalars):
    for sweep_index in range(1, SWEEPS - 1):
        lo, hi = exchange_halos(fwd, bwd)
        potential, fwd, bwd = sweep_call(
            False, potential, False, lo, hi, partner, targets, tmat, scalars
        )
    lo, hi = exchange_halos(fwd, bwd)
    return sweep_call(True, potential, False, lo, hi, partner, targets, tmat, scalars)


def butterfly_sum(x, axis):
    count = lax.axis_size(axis)
    step = 1
    while step < count:
        radix = 2
        total = x
        for part in range(1, radix):
            pairs = [
                (k, (k // (step * radix)) * step * radix + ((k // step) % radix ^ part) * step + k % step)
                for k in range(count)
            ]
            total = total + lax.ppermute(x, axis, pairs)
        x = total
        step *= radix
    return x


def swap_over_y(block, mesh_shape):
    bands, domains = mesh_shape
    lanes = domains // 2
    def index(y, rest):
        return (y // 2) * domains + (y % 2) * lanes + rest
    ring = 2 * bands
    def shift(direction):
        return [
            (index(y, rest), index((y + direction) % ring, rest))
            for y in range(ring)
            for rest in range(lanes)
        ]
    half = block.shape[0] // 2
    axes = ("band", "domain")
    plus = lax.ppermute(block[:half], axes, shift(1))
    minus = lax.ppermute(block[half:], axes, shift(-1))
    return plus, minus, lambda plus, minus: jnp.concatenate(
        [lax.ppermute(plus, axes, shift(1)), lax.ppermute(minus, axes, shift(-1))], axis=0
    )


def pair_sums(block, targets):
    part = block.astype(jnp.float32)
    return jnp.sum(part[:, None] * targets[None], axis=(2, 3))


def mean_term(block, means):
    part = block.astype(jnp.float32)
    total = None
    for i in range(block.shape[0]):
        term = means[i][:, None, None] * part[i][None]
        total = term if total is None else total + term
    return total


def body(targets, partner_pool, owners, warm_start):
    row_count = targets.shape[1]
    cell_count = GX * GY * GZ
    domain = lax.axis_index("domain")
    band = lax.axis_index("band")
    y0 = (domain * row_count) % GY
    s_own = jnp.where(owners[0] == band, 0, 1).astype(jnp.int32)
    s_rem = 1 - s_own
    own_block = lax.dynamic_slice_in_dim(partner_pool, s_own * ORB, ORB, 0)
    tmat = (circulant(GY), circulant(targets.shape[2]))
    own_scalars = jnp.stack([y0, s_own, s_own * ORB]).astype(jnp.int32)
    rem_scalars = jnp.stack([y0, s_rem, jnp.zeros((), jnp.int32)]).astype(jnp.int32)

    own_halos = exchange_halos(*warm_halos(warm_start, s_own, row_count))
    plus, minus, finish_swap = swap_over_y(
        own_block, (lax.axis_size("band"), lax.axis_size("domain"))
    )
    rem_sends, own_halos, plus, minus = lax.optimization_barrier(
        (warm_halos(warm_start, s_rem, row_count), own_halos, plus, minus)
    )
    rem_halos = exchange_halos(*rem_sends)
    rem_block = finish_swap(plus, minus)
    potential, fwd, bwd = sweep_call(
        False, warm_start, True, *own_halos, partner_pool, targets, tmat, own_scalars
    )
    rem_state = sweep_call(
        False, warm_start, True, *rem_halos, rem_block, targets, tmat, rem_scalars
    )

    sums = jnp.stack([pair_sums(own_block, targets), pair_sums(rem_block, targets)])
    means = butterfly_sum(sums, "domain") / cell_count

    own_acc = finish_stream(potential, fwd, bwd, partner_pool, targets, tmat, own_scalars)
    rem_acc = finish_stream(*rem_state, rem_block, targets, tmat, rem_scalars)
    correction = mean_term(own_block, means[0]) + mean_term(rem_block, means[1])
    return (0.5 * coupling) * correction - (own_acc + rem_acc)


def solution(mesh):
    return jax.shard_map(
        body,
        mesh=mesh,
        in_specs=(
            P("band", "domain", None),
            P("band", "domain", None),
            P(),
            P(None, None, "band", "domain", None),
        ),
        out_specs=P("band", "domain", None),
        check_vma=False,
    )
```

```python
import functools
import math

import jax
import jax.numpy as jnp
from jax import lax
from jax.experimental import pallas as pl
from jax.experimental.pallas import tpu as pltpu
from jax.sharding import PartitionSpec as P

ORB = 8
STEPS = 2
SWEEPS = 3
GX = 192
GY = 192
GZ = 192


coupling = 4.0 * math.pi


def circulant(width):
    a = lax.broadcasted_iota(jnp.int32, (width, width), 0)
    b = lax.broadcasted_iota(jnp.int32, (width, width), 1)
    gap = (a - b + width) % width
    return ((gap == 1) | (gap == width - 1)).astype(jnp.bfloat16)


def stencil(y0, v, lo, hi, q, t_ref, wide):
    row_count = v.shape[0]
    halo = lo.shape[0]
    wide[0:halo, :] = lo
    wide[halo : halo + row_count, :] = v
    wide[halo + row_count : 2 * halo + row_count, :] = hi
    beside = wide[0:row_count, :] + wide[2 * halo : 2 * halo + row_count, :]
    down = wide[halo - 1 : halo - 1 + row_count, :]
    up = wide[halo + 1 : halo + 1 + row_count, :]
    down_wrap = wide[2 * halo - 1 : 2 * halo - 1 + row_count, :]
    up_wrap = wide[1 : 1 + row_count, :]
    y = lax.broadcasted_iota(jnp.int32, v.shape, 0) + y0
    for _ in range((row_count + GY - 2) // GY):
        y = jnp.where(y >= GY, y - GY, y)
    beside = beside + jnp.where(y == 0, down_wrap, down)
    beside = beside + jnp.where(y == GY - 1, up_wrap, up)
    high = v.astype(jnp.bfloat16)
    low = (v - high.astype(jnp.float32)).astype(jnp.bfloat16)
    tmat = t_ref[...]
    beside = beside + jnp.dot(high, tmat, preferred_element_type=jnp.float32)
    beside = beside + jnp.dot(low, tmat, preferred_element_type=jnp.float32)
    return (beside + coupling * q) * (1.0 / 6.0)


def sweep_kernel(final, sc_ref, v_ref, lo_ref, hi_ref, p_ref, t_ref, c_ref, *rest):
    y0 = sc_ref[0]
    part = p_ref[...].astype(jnp.float32)
    row_count = part.shape[0]
    halo = lo_ref.shape[-2]
    if final:
        acc_ref, wide = rest

        @pl.when(pl.program_id(0) == 0)
        def _():
            acc_ref[...] = jnp.zeros_like(acc_ref)

    else:
        out_ref, fwd_ref, bwd_ref, wide = rest
    for j in range(v_ref.shape[0]):
        q = part * t_ref[j]
        new = stencil(
            y0,
            v_ref[j].astype(jnp.float32),
            lo_ref[j].astype(jnp.float32),
            hi_ref[j].astype(jnp.float32),
            q,
            c_ref,
            wide,
        )
        if final:
            acc_ref[j] = acc_ref[j] + new * part
        else:
            out_ref[j] = new
            fwd_ref[j] = new[row_count - halo : row_count].astype(jnp.bfloat16)
            bwd_ref[j] = new[0:halo].astype(jnp.bfloat16)


def sweep_call(final, v, from_warm, lo, hi, partner, targets, tmat, scalars):
    orb, tgt, halo, width = lo.shape
    row_count = targets.shape[1]
    if from_warm:
        v_spec = pl.BlockSpec(
            (None, None, tgt, row_count, width), lambda i, sc: (sc[1], i, 0, 0, 0)
        )
    else:
        v_spec = pl.BlockSpec((None, tgt, row_count, width), lambda i, sc: (i, 0, 0, 0))
    h_spec = pl.BlockSpec((None, tgt, halo, width), lambda i, sc: (i, 0, 0, 0))
    p_spec = pl.BlockSpec((None, row_count, width), lambda i, sc: (sc[2] + i, 0, 0))
    t_spec = pl.BlockSpec((tgt, row_count, width), lambda i, sc: (0, 0, 0))
    c_spec = pl.BlockSpec((width, width), lambda i, sc: (0, 0))
    cells = orb * tgt * row_count * width
    if final:
        out_shape = jax.ShapeDtypeStruct((tgt, row_count, width), jnp.float32)
        out_specs = pl.BlockSpec((tgt, row_count, width), lambda i, sc: (0, 0, 0))
        out_bytes = tgt * row_count * width * 4
    else:
        out_shape = (
            jax.ShapeDtypeStruct((orb, tgt, row_count, width), jnp.float32),
            jax.ShapeDtypeStruct((orb, tgt, halo, width), jnp.bfloat16),
            jax.ShapeDtypeStruct((orb, tgt, halo, width), jnp.bfloat16),
        )
        out_specs = (
            pl.BlockSpec((None, tgt, row_count, width), lambda i, sc: (i, 0, 0, 0)),
            h_spec,
            h_spec,
        )
        out_bytes = cells * 4 + 2 * orb * tgt * halo * width * 2
    in_bytes = (
        cells * v.dtype.itemsize
        + 2 * orb * tgt * halo * width * 2
        + orb * row_count * width * 2
        + tgt * row_count * width * 4
    )
    grid_spec = pltpu.PrefetchScalarGridSpec(
        num_scalar_prefetch=1,
        grid=(orb,),
        in_specs=[v_spec, h_spec, h_spec, p_spec, t_spec, c_spec],
        out_specs=out_specs,
        scratch_shapes=[pltpu.VMEM((row_count + 2 * halo, width), jnp.float32)],
    )
    return pl.pallas_call(
        functools.partial(sweep_kernel, final),
        grid_spec=grid_spec,
        out_shape=out_shape,
        compiler_params=pltpu.CompilerParams(dimension_semantics=("arbitrary",)),
        cost_estimate=pl.CostEstimate(
            flops=cells * (4 * width + 24),
            transcendentals=0,
            bytes_accessed=in_bytes + out_bytes,
        ),
    )(scalars, v, lo, hi, partner, targets, tmat)


def exchange_halos(fwd, bwd):
    count = lax.axis_size("domain")
    forward = [(k, (k + 1) % count) for k in range(count)]
    backward = [((k + 1) % count, k) for k in range(count)]
    return lax.ppermute(fwd, "domain", forward), lax.ppermute(bwd, "domain", backward)


def warm_halos(warm_start, s, row_count):
    warm_block = lax.dynamic_index_in_dim(warm_start, s, 0, keepdims=False)
    return warm_block[:, :, row_count - GY :], warm_block[:, :, :GY]


def finish_stream(potential, fwd, bwd, partner, targets, tmat, scalars):
    for sweep_index in range(1, SWEEPS - 1):
        lo, hi = exchange_halos(fwd, bwd)
        potential, fwd, bwd = sweep_call(
            False, potential, False, lo, hi, partner, targets, tmat, scalars
        )
    lo, hi = exchange_halos(fwd, bwd)
    return sweep_call(True, potential, False, lo, hi, partner, targets, tmat, scalars)


def butterfly_sum(x, axis):
    count = lax.axis_size(axis)
    step = 1
    while step < count:
        radix = 2
        total = x
        for part in range(1, radix):
            pairs = [
                (k, (k // (step * radix)) * step * radix + ((k // step) % radix ^ part) * step + k % step)
                for k in range(count)
            ]
            total = total + lax.ppermute(x, axis, pairs)
        x = total
        step *= radix
    return x


def swap_over_y(block, mesh_shape):
    bands, domains = mesh_shape
    lanes = domains // 2
    def index(y, rest):
        return (y // 2) * domains + (y % 2) * lanes + rest
    ring = 2 * bands
    def shift(direction):
        return [
            (index(y, rest), index((y + direction) % ring, rest))
            for y in range(ring)
            for rest in range(lanes)
        ]
    axes = ("band", "domain")
    directions = [1, -1, 1, -1]

    def hop(pieces, offset):
        return [
            lax.ppermute(piece, axes, shift(directions[offset + k]))
            for k, piece in enumerate(pieces)
        ]

    return jnp.split(block, len(directions), axis=0), hop


def pair_sums(block, targets):
    part = block.astype(jnp.float32)
    return jnp.sum(part[:, None] * targets[None], axis=(2, 3))


def mean_term(block, means):
    part = block.astype(jnp.float32)
    total = None
    for i in range(block.shape[0]):
        term = means[i][:, None, None] * part[i][None]
        total = term if total is None else total + term
    return total


def body(targets, partner_pool, owners, warm_start):
    row_count = targets.shape[1]
    cell_count = GX * GY * GZ
    domain = lax.axis_index("domain")
    band = lax.axis_index("band")
    y0 = (domain * row_count) % GY
    s_own = jnp.where(owners[0] == band, 0, 1).astype(jnp.int32)
    s_rem = 1 - s_own
    own_block = lax.dynamic_slice_in_dim(partner_pool, s_own * ORB, ORB, 0)
    tmat = circulant(targets.shape[2])
    own_scalars = jnp.stack([y0, s_own, s_own * ORB]).astype(jnp.int32)
    rem_scalars = jnp.stack([y0, s_rem, jnp.zeros((), jnp.int32)]).astype(jnp.int32)

    own_halos = exchange_halos(*warm_halos(warm_start, s_own, row_count))
    pieces, hop = swap_over_y(own_block, (lax.axis_size("band"), lax.axis_size("domain")))
    early = hop(pieces[:2], 0)
    rem_sends, own_halos, early, late = lax.optimization_barrier(
        (warm_halos(warm_start, s_rem, row_count), own_halos, early, pieces[2:])
    )
    rem_halos = exchange_halos(*rem_sends)
    early = hop(early, 0)
    late = hop(late, 2)
    potential, fwd, bwd = sweep_call(
        False, warm_start, True, *own_halos, partner_pool, targets, tmat, own_scalars
    )
    late, potential = lax.optimization_barrier((late, potential))
    rem_block = jnp.concatenate(early + hop(late, 2), axis=0)
    rem_state = sweep_call(
        False, warm_start, True, *rem_halos, rem_block, targets, tmat, rem_scalars
    )

    sums = jnp.stack([pair_sums(own_block, targets), pair_sums(rem_block, targets)])
    means = butterfly_sum(sums, "domain") / cell_count

    own_acc = finish_stream(potential, fwd, bwd, partner_pool, targets, tmat, own_scalars)
    rem_acc = finish_stream(*rem_state, rem_block, targets, tmat, rem_scalars)
    correction = mean_term(own_block, means[0]) + mean_term(rem_block, means[1])
    return (0.5 * coupling) * correction - (own_acc + rem_acc)


def solution(mesh):
    return jax.shard_map(
        body,
        mesh=mesh,
        in_specs=(
            P("band", "domain", None),
            P("band", "domain", None),
            P(),
            P(None, None, "band", "domain", None),
        ),
        out_specs=P("band", "domain", None),
        check_vma=False,
    )
```

```python
import functools
import math

import jax
import jax.numpy as jnp
from jax import lax
from jax.experimental import pallas as pl
from jax.experimental.pallas import tpu as pltpu
from jax.sharding import PartitionSpec as P

ORB = 8
STEPS = 2
SWEEPS = 3
GX = 192
GY = 192
GZ = 192


coupling = 4.0 * math.pi


def circulant(width):
    a = lax.broadcasted_iota(jnp.int32, (width, width), 0)
    b = lax.broadcasted_iota(jnp.int32, (width, width), 1)
    gap = (a - b + width) % width
    return ((gap == 1) | (gap == width - 1)).astype(jnp.bfloat16)


def stencil(y0, v, lo, hi, q, t_ref, wide):
    row_count = v.shape[0]
    halo = lo.shape[0]
    wide[0:halo, :] = lo
    wide[halo : halo + row_count, :] = v
    wide[halo + row_count : 2 * halo + row_count, :] = hi
    beside = wide[0:row_count, :] + wide[2 * halo : 2 * halo + row_count, :]
    down = wide[halo - 1 : halo - 1 + row_count, :]
    up = wide[halo + 1 : halo + 1 + row_count, :]
    down_wrap = wide[2 * halo - 1 : 2 * halo - 1 + row_count, :]
    up_wrap = wide[1 : 1 + row_count, :]
    y = lax.broadcasted_iota(jnp.int32, v.shape, 0) + y0
    for _ in range((row_count + GY - 2) // GY):
        y = jnp.where(y >= GY, y - GY, y)
    beside = beside + jnp.where(y == 0, down_wrap, down)
    beside = beside + jnp.where(y == GY - 1, up_wrap, up)
    high = v.astype(jnp.bfloat16)
    low = (v - high.astype(jnp.float32)).astype(jnp.bfloat16)
    tmat = t_ref[...]
    beside = beside + jnp.dot(high, tmat, preferred_element_type=jnp.float32)
    beside = beside + jnp.dot(low, tmat, preferred_element_type=jnp.float32)
    return (beside + coupling * q) * (1.0 / 6.0)


def sweep_kernel(final, has_init, sc_ref, v_ref, lo_ref, hi_ref, p_ref, t_ref, c_ref, *rest):
    y0 = sc_ref[0]
    part = p_ref[...].astype(jnp.float32)
    row_count = part.shape[0]
    halo = lo_ref.shape[-2]
    if final:
        if has_init:
            m_ref, init_ref, acc_ref, wide = rest
        else:
            m_ref, acc_ref, wide = rest

        @pl.when(pl.program_id(0) == 0)
        def _():
            if has_init:
                acc_ref[...] = init_ref[...]
            else:
                acc_ref[...] = jnp.zeros_like(acc_ref)

    else:
        out_ref, fwd_ref, bwd_ref, wide = rest
    for j in range(v_ref.shape[0]):
        q = part * t_ref[j]
        new = stencil(
            y0,
            v_ref[j].astype(jnp.float32),
            lo_ref[j].astype(jnp.float32),
            hi_ref[j].astype(jnp.float32),
            q,
            c_ref,
            wide,
        )
        if final:
            shift = (0.5 * coupling) * m_ref[pl.program_id(0), j]
            acc_ref[j] = acc_ref[j] - (new - shift) * part
        else:
            out_ref[j] = new
            fwd_ref[j] = new[row_count - halo : row_count].astype(jnp.bfloat16)
            bwd_ref[j] = new[0:halo].astype(jnp.bfloat16)


def sweep_call(final, v, from_warm, lo, hi, partner, targets, tmat, scalars, means=None, init=None):
    orb, tgt, halo, width = lo.shape
    row_count = targets.shape[1]
    if from_warm:
        v_spec = pl.BlockSpec(
            (None, None, tgt, row_count, width), lambda i, sc: (sc[1], i, 0, 0, 0)
        )
    else:
        v_spec = pl.BlockSpec((None, tgt, row_count, width), lambda i, sc: (i, 0, 0, 0))
    h_spec = pl.BlockSpec((None, tgt, halo, width), lambda i, sc: (i, 0, 0, 0))
    p_spec = pl.BlockSpec((None, row_count, width), lambda i, sc: (sc[2] + i, 0, 0))
    t_spec = pl.BlockSpec((tgt, row_count, width), lambda i, sc: (0, 0, 0))
    c_spec = pl.BlockSpec((width, width), lambda i, sc: (0, 0))
    cells = orb * tgt * row_count * width
    in_specs = [v_spec, h_spec, h_spec, p_spec, t_spec, c_spec]
    extra = []
    if final:
        in_specs.append(pl.BlockSpec(memory_space=pltpu.SMEM))
        extra.append(means)
        if init is not None:
            in_specs.append(pl.BlockSpec((tgt, row_count, width), lambda i, sc: (0, 0, 0)))
            extra.append(init)
        out_shape = jax.ShapeDtypeStruct((tgt, row_count, width), jnp.float32)
        out_specs = pl.BlockSpec((tgt, row_count, width), lambda i, sc: (0, 0, 0))
        out_bytes = tgt * row_count * width * 4
    else:
        out_shape = (
            jax.ShapeDtypeStruct((orb, tgt, row_count, width), jnp.float32),
            jax.ShapeDtypeStruct((orb, tgt, halo, width), jnp.bfloat16),
            jax.ShapeDtypeStruct((orb, tgt, halo, width), jnp.bfloat16),
        )
        out_specs = (
            pl.BlockSpec((None, tgt, row_count, width), lambda i, sc: (i, 0, 0, 0)),
            h_spec,
            h_spec,
        )
        out_bytes = cells * 4 + 2 * orb * tgt * halo * width * 2
    in_bytes = (
        cells * v.dtype.itemsize
        + 2 * orb * tgt * halo * width * 2
        + orb * row_count * width * 2
        + tgt * row_count * width * 4
    )
    grid_spec = pltpu.PrefetchScalarGridSpec(
        num_scalar_prefetch=1,
        grid=(orb,),
        in_specs=in_specs,
        out_specs=out_specs,
        scratch_shapes=[pltpu.VMEM((row_count + 2 * halo, width), jnp.float32)],
    )
    return pl.pallas_call(
        functools.partial(sweep_kernel, final, init is not None),
        grid_spec=grid_spec,
        out_shape=out_shape,
        compiler_params=pltpu.CompilerParams(dimension_semantics=("arbitrary",)),
        cost_estimate=pl.CostEstimate(
            flops=cells * (4 * width + 24),
            transcendentals=0,
            bytes_accessed=in_bytes + out_bytes,
        ),
    )(scalars, v, lo, hi, partner, targets, tmat, *extra)


def exchange_halos(fwd, bwd):
    count = lax.axis_size("domain")
    forward = [(k, (k + 1) % count) for k in range(count)]
    backward = [((k + 1) % count, k) for k in range(count)]
    return lax.ppermute(fwd, "domain", forward), lax.ppermute(bwd, "domain", backward)


def warm_halos(warm_start, s, row_count):
    warm_block = lax.dynamic_index_in_dim(warm_start, s, 0, keepdims=False)
    return warm_block[:, :, row_count - GY :], warm_block[:, :, :GY]


def finish_stream(potential, fwd, bwd, partner, targets, tmat, scalars, means, init):
    for sweep_index in range(1, SWEEPS - 1):
        lo, hi = exchange_halos(fwd, bwd)
        potential, fwd, bwd = sweep_call(
            False, potential, False, lo, hi, partner, targets, tmat, scalars
        )
    lo, hi = exchange_halos(fwd, bwd)
    return sweep_call(
        True, potential, False, lo, hi, partner, targets, tmat, scalars, means, init
    )


def butterfly_sum(x, axis):
    count = lax.axis_size(axis)
    step = 1
    while step < count:
        radix = 2
        total = x
        for part in range(1, radix):
            pairs = [
                (k, (k // (step * radix)) * step * radix + ((k // step) % radix ^ part) * step + k % step)
                for k in range(count)
            ]
            total = total + lax.ppermute(x, axis, pairs)
        x = total
        step *= radix
    return x


def swap_over_y(block, mesh_shape):
    bands, domains = mesh_shape
    lanes = domains // 2
    def index(y, rest):
        return (y // 2) * domains + (y % 2) * lanes + rest
    ring = 2 * bands
    def shift(direction):
        return [
            (index(y, rest), index((y + direction) % ring, rest))
            for y in range(ring)
            for rest in range(lanes)
        ]
    half = block.shape[0] // 2
    axes = ("band", "domain")
    plus = lax.ppermute(block[:half], axes, shift(1))
    minus = lax.ppermute(block[half:], axes, shift(-1))
    return plus, minus, lambda plus, minus: jnp.concatenate(
        [lax.ppermute(plus, axes, shift(1)), lax.ppermute(minus, axes, shift(-1))], axis=0
    )


def pair_sums(block, targets):
    part = block.astype(jnp.float32)
    return jnp.sum(part[:, None] * targets[None], axis=(2, 3))


def body(targets, partner_pool, owners, warm_start):
    row_count = targets.shape[1]
    cell_count = GX * GY * GZ
    domain = lax.axis_index("domain")
    band = lax.axis_index("band")
    y0 = (domain * row_count) % GY
    s_own = jnp.where(owners[0] == band, 0, 1).astype(jnp.int32)
    s_rem = 1 - s_own
    own_block = lax.dynamic_slice_in_dim(partner_pool, s_own * ORB, ORB, 0)
    tmat = circulant(targets.shape[2])
    own_scalars = jnp.stack([y0, s_own, s_own * ORB]).astype(jnp.int32)
    rem_scalars = jnp.stack([y0, s_rem, jnp.zeros((), jnp.int32)]).astype(jnp.int32)

    own_halos = exchange_halos(*warm_halos(warm_start, s_own, row_count))
    plus, minus, finish_swap = swap_over_y(
        own_block, (lax.axis_size("band"), lax.axis_size("domain"))
    )
    rem_sends, own_halos, plus, minus = lax.optimization_barrier(
        (warm_halos(warm_start, s_rem, row_count), own_halos, plus, minus)
    )
    rem_halos = exchange_halos(*rem_sends)
    rem_block = finish_swap(plus, minus)
    potential, fwd, bwd = sweep_call(
        False, warm_start, True, *own_halos, partner_pool, targets, tmat, own_scalars
    )
    rem_state = sweep_call(
        False, warm_start, True, *rem_halos, rem_block, targets, tmat, rem_scalars
    )

    sums = jnp.stack([pair_sums(own_block, targets), pair_sums(rem_block, targets)])
    means = butterfly_sum(sums, "domain") / cell_count

    own_acc = finish_stream(
        potential, fwd, bwd, partner_pool, targets, tmat, own_scalars, means[0], None
    )
    return finish_stream(
        *rem_state, rem_block, targets, tmat, rem_scalars, means[1], own_acc
    )


def solution(mesh):
    return jax.shard_map(
        body,
        mesh=mesh,
        in_specs=(
            P("band", "domain", None),
            P("band", "domain", None),
            P(),
            P(None, None, "band", "domain", None),
        ),
        out_specs=P("band", "domain", None),
        check_vma=False,
    )
```

```python
import functools
import math

import jax
import jax.numpy as jnp
from jax import lax
from jax.experimental import pallas as pl
from jax.experimental.pallas import tpu as pltpu
from jax.sharding import PartitionSpec as P

ORB = 8
STEPS = 2
SWEEPS = 3
GX = 192
GY = 192
GZ = 192


coupling = 4.0 * math.pi
PER_STEP = 2


def circulant(width):
    a = lax.broadcasted_iota(jnp.int32, (width, width), 0)
    b = lax.broadcasted_iota(jnp.int32, (width, width), 1)
    gap = (a - b + width) % width
    return ((gap == 1) | (gap == width - 1)).astype(jnp.bfloat16)


def stencil(y0, v, lo, hi, q, t_ref, wide):
    row_count = v.shape[0]
    halo = lo.shape[0]
    wide[0:halo, :] = lo
    wide[halo : halo + row_count, :] = v
    wide[halo + row_count : 2 * halo + row_count, :] = hi
    beside = wide[0:row_count, :] + wide[2 * halo : 2 * halo + row_count, :]
    down = wide[halo - 1 : halo - 1 + row_count, :]
    up = wide[halo + 1 : halo + 1 + row_count, :]
    down_wrap = wide[2 * halo - 1 : 2 * halo - 1 + row_count, :]
    up_wrap = wide[1 : 1 + row_count, :]
    y = lax.broadcasted_iota(jnp.int32, v.shape, 0) + y0
    for _ in range((row_count + GY - 2) // GY):
        y = jnp.where(y >= GY, y - GY, y)
    beside = beside + jnp.where(y == 0, down_wrap, down)
    beside = beside + jnp.where(y == GY - 1, up_wrap, up)
    high = v.astype(jnp.bfloat16)
    low = (v - high.astype(jnp.float32)).astype(jnp.bfloat16)
    tmat = t_ref[...]
    beside = beside + jnp.dot(high, tmat, preferred_element_type=jnp.float32)
    beside = beside + jnp.dot(low, tmat, preferred_element_type=jnp.float32)
    return (beside + coupling * q) * (1.0 / 6.0)


def sweep_kernel(final, has_init, sc_ref, v_ref, lo_ref, hi_ref, p_ref, t_ref, c_ref, *rest):
    y0 = sc_ref[0]
    pb = p_ref.shape[0]
    row_count = p_ref.shape[1]
    halo = lo_ref.shape[-2]
    if final:
        if has_init:
            m_ref, init_ref, acc_ref, wide = rest
        else:
            m_ref, acc_ref, wide = rest

        @pl.when(pl.program_id(0) == 0)
        def _():
            if has_init:
                acc_ref[...] = init_ref[...]
            else:
                acc_ref[...] = jnp.zeros_like(acc_ref)

    else:
        out_ref, fwd_ref, bwd_ref, wide = rest
    for k in range(pb):
        part = p_ref[k].astype(jnp.float32)
        for j in range(v_ref.shape[1]):
            q = part * t_ref[j]
            new = stencil(
                y0,
                v_ref[k, j].astype(jnp.float32),
                lo_ref[k, j].astype(jnp.float32),
                hi_ref[k, j].astype(jnp.float32),
                q,
                c_ref,
                wide,
            )
            if final:
                shift = (0.5 * coupling) * m_ref[pl.program_id(0) * pb + k, j]
                acc_ref[j] = acc_ref[j] - (new - shift) * part
            else:
                out_ref[k, j] = new
                fwd_ref[k, j] = new[row_count - halo : row_count].astype(jnp.bfloat16)
                bwd_ref[k, j] = new[0:halo].astype(jnp.bfloat16)


def sweep_call(final, v, from_warm, lo, hi, partner, targets, tmat, scalars, means=None, init=None):
    orb, tgt, halo, width = lo.shape
    row_count = targets.shape[1]
    pb = PER_STEP
    if from_warm:
        v_spec = pl.BlockSpec(
            (None, pb, tgt, row_count, width), lambda i, sc: (sc[1], i, 0, 0, 0)
        )
    else:
        v_spec = pl.BlockSpec((pb, tgt, row_count, width), lambda i, sc: (i, 0, 0, 0))
    h_spec = pl.BlockSpec((pb, tgt, halo, width), lambda i, sc: (i, 0, 0, 0))
    p_spec = pl.BlockSpec((pb, row_count, width), lambda i, sc: (sc[2] // pb + i, 0, 0))
    t_spec = pl.BlockSpec((tgt, row_count, width), lambda i, sc: (0, 0, 0))
    c_spec = pl.BlockSpec((width, width), lambda i, sc: (0, 0))
    cells = orb * tgt * row_count * width
    in_specs = [v_spec, h_spec, h_spec, p_spec, t_spec, c_spec]
    extra = []
    if final:
        in_specs.append(pl.BlockSpec(memory_space=pltpu.SMEM))
        extra.append(means)
        if init is not None:
            in_specs.append(pl.BlockSpec((tgt, row_count, width), lambda i, sc: (0, 0, 0)))
            extra.append(init)
        out_shape = jax.ShapeDtypeStruct((tgt, row_count, width), jnp.float32)
        out_specs = pl.BlockSpec((tgt, row_count, width), lambda i, sc: (0, 0, 0))
        out_bytes = tgt * row_count * width * 4
    else:
        out_shape = (
            jax.ShapeDtypeStruct((orb, tgt, row_count, width), jnp.float32),
            jax.ShapeDtypeStruct((orb, tgt, halo, width), jnp.bfloat16),
            jax.ShapeDtypeStruct((orb, tgt, halo, width), jnp.bfloat16),
        )
        out_specs = (
            pl.BlockSpec((pb, tgt, row_count, width), lambda i, sc: (i, 0, 0, 0)),
            h_spec,
            h_spec,
        )
        out_bytes = cells * 4 + 2 * orb * tgt * halo * width * 2
    in_bytes = (
        cells * v.dtype.itemsize
        + 2 * orb * tgt * halo * width * 2
        + orb * row_count * width * 2
        + tgt * row_count * width * 4
    )
    grid_spec = pltpu.PrefetchScalarGridSpec(
        num_scalar_prefetch=1,
        grid=(orb // pb,),
        in_specs=in_specs,
        out_specs=out_specs,
        scratch_shapes=[pltpu.VMEM((row_count + 2 * halo, width), jnp.float32)],
    )
    return pl.pallas_call(
        functools.partial(sweep_kernel, final, init is not None),
        grid_spec=grid_spec,
        out_shape=out_shape,
        compiler_params=pltpu.CompilerParams(dimension_semantics=("arbitrary",)),
        cost_estimate=pl.CostEstimate(
            flops=cells * (4 * width + 24),
            transcendentals=0,
            bytes_accessed=in_bytes + out_bytes,
        ),
    )(scalars, v, lo, hi, partner, targets, tmat, *extra)


def exchange_halos(fwd, bwd):
    count = lax.axis_size("domain")
    forward = [(k, (k + 1) % count) for k in range(count)]
    backward = [((k + 1) % count, k) for k in range(count)]
    return lax.ppermute(fwd, "domain", forward), lax.ppermute(bwd, "domain", backward)


def warm_halos(warm_start, s, row_count):
    warm_block = lax.dynamic_index_in_dim(warm_start, s, 0, keepdims=False)
    return warm_block[:, :, row_count - GY :], warm_block[:, :, :GY]


def finish_stream(potential, fwd, bwd, partner, targets, tmat, scalars, means, init):
    for sweep_index in range(1, SWEEPS - 1):
        lo, hi = exchange_halos(fwd, bwd)
        potential, fwd, bwd = sweep_call(
            False, potential, False, lo, hi, partner, targets, tmat, scalars
        )
    lo, hi = exchange_halos(fwd, bwd)
    return sweep_call(
        True, potential, False, lo, hi, partner, targets, tmat, scalars, means, init
    )


def butterfly_sum(x, axis):
    count = lax.axis_size(axis)
    step = 1
    while step < count:
        radix = 2
        total = x
        for part in range(1, radix):
            pairs = [
                (k, (k // (step * radix)) * step * radix + ((k // step) % radix ^ part) * step + k % step)
                for k in range(count)
            ]
            total = total + lax.ppermute(x, axis, pairs)
        x = total
        step *= radix
    return x


def swap_over_y(block, mesh_shape):
    bands, domains = mesh_shape
    lanes = domains // 2
    def index(y, rest):
        return (y // 2) * domains + (y % 2) * lanes + rest
    ring = 2 * bands
    def shift(direction):
        return [
            (index(y, rest), index((y + direction) % ring, rest))
            for y in range(ring)
            for rest in range(lanes)
        ]
    half = block.shape[0] // 2
    axes = ("band", "domain")
    plus = lax.ppermute(block[:half], axes, shift(1))
    minus = lax.ppermute(block[half:], axes, shift(-1))
    return plus, minus, lambda plus, minus: jnp.concatenate(
        [lax.ppermute(plus, axes, shift(1)), lax.ppermute(minus, axes, shift(-1))], axis=0
    )


def pair_sums(block, targets):
    part = block.astype(jnp.float32)
    return jnp.sum(part[:, None] * targets[None], axis=(2, 3))


def body(targets, partner_pool, owners, warm_start):
    row_count = targets.shape[1]
    cell_count = GX * GY * GZ
    domain = lax.axis_index("domain")
    band = lax.axis_index("band")
    y0 = (domain * row_count) % GY
    s_own = jnp.where(owners[0] == band, 0, 1).astype(jnp.int32)
    s_rem = 1 - s_own
    own_block = lax.dynamic_slice_in_dim(partner_pool, s_own * ORB, ORB, 0)
    tmat = circulant(targets.shape[2])
    own_scalars = jnp.stack([y0, s_own, s_own * ORB]).astype(jnp.int32)
    rem_scalars = jnp.stack([y0, s_rem, jnp.zeros((), jnp.int32)]).astype(jnp.int32)

    own_halos = exchange_halos(*warm_halos(warm_start, s_own, row_count))
    plus, minus, finish_swap = swap_over_y(
        own_block, (lax.axis_size("band"), lax.axis_size("domain"))
    )
    rem_sends, own_halos, plus, minus = lax.optimization_barrier(
        (warm_halos(warm_start, s_rem, row_count), own_halos, plus, minus)
    )
    rem_halos = exchange_halos(*rem_sends)
    rem_block = finish_swap(plus, minus)
    potential, fwd, bwd = sweep_call(
        False, warm_start, True, *own_halos, partner_pool, targets, tmat, own_scalars
    )
    rem_state = sweep_call(
        False, warm_start, True, *rem_halos, rem_block, targets, tmat, rem_scalars
    )

    sums = jnp.stack([pair_sums(own_block, targets), pair_sums(rem_block, targets)])
    means = butterfly_sum(sums, "domain") / cell_count

    own_acc = finish_stream(
        potential, fwd, bwd, partner_pool, targets, tmat, own_scalars, means[0], None
    )
    return finish_stream(
        *rem_state, rem_block, targets, tmat, rem_scalars, means[1], own_acc
    )


def solution(mesh):
    return jax.shard_map(
        body,
        mesh=mesh,
        in_specs=(
            P("band", "domain", None),
            P("band", "domain", None),
            P(),
            P(None, None, "band", "domain", None),
        ),
        out_specs=P("band", "domain", None),
        check_vma=False,
    )
```

```python
import functools
import math

import jax
import jax.numpy as jnp
from jax import lax
from jax.experimental import pallas as pl
from jax.experimental.pallas import tpu as pltpu
from jax.sharding import PartitionSpec as P

ORB = 8
STEPS = 2
SWEEPS = 3
GX = 192
GY = 192
GZ = 192


coupling = 4.0 * math.pi
PER_STEP = 4


def circulant(width):
    a = lax.broadcasted_iota(jnp.int32, (width, width), 0)
    b = lax.broadcasted_iota(jnp.int32, (width, width), 1)
    gap = (a - b + width) % width
    return ((gap == 1) | (gap == width - 1)).astype(jnp.bfloat16)


def stencil(y0, v, lo, hi, q, t_ref, wide):
    row_count = v.shape[0]
    halo = lo.shape[0]
    wide[0:halo, :] = lo
    wide[halo : halo + row_count, :] = v
    wide[halo + row_count : 2 * halo + row_count, :] = hi
    beside = wide[0:row_count, :] + wide[2 * halo : 2 * halo + row_count, :]
    down = wide[halo - 1 : halo - 1 + row_count, :]
    up = wide[halo + 1 : halo + 1 + row_count, :]
    down_wrap = wide[2 * halo - 1 : 2 * halo - 1 + row_count, :]
    up_wrap = wide[1 : 1 + row_count, :]
    y = lax.broadcasted_iota(jnp.int32, v.shape, 0) + y0
    for _ in range((row_count + GY - 2) // GY):
        y = jnp.where(y >= GY, y - GY, y)
    beside = beside + jnp.where(y == 0, down_wrap, down)
    beside = beside + jnp.where(y == GY - 1, up_wrap, up)
    high = v.astype(jnp.bfloat16)
    low = (v - high.astype(jnp.float32)).astype(jnp.bfloat16)
    tmat = t_ref[...]
    beside = beside + jnp.dot(high, tmat, preferred_element_type=jnp.float32)
    beside = beside + jnp.dot(low, tmat, preferred_element_type=jnp.float32)
    return (beside + coupling * q) * (1.0 / 6.0)


def sweep_kernel(final, has_init, sc_ref, v_ref, lo_ref, hi_ref, p_ref, t_ref, c_ref, *rest):
    y0 = sc_ref[0]
    pb = p_ref.shape[0]
    row_count = p_ref.shape[1]
    halo = lo_ref.shape[-2]
    if final:
        if has_init:
            m_ref, init_ref, acc_ref, wide = rest
        else:
            m_ref, acc_ref, wide = rest

        @pl.when(pl.program_id(0) == 0)
        def _():
            if has_init:
                acc_ref[...] = init_ref[...]
            else:
                acc_ref[...] = jnp.zeros_like(acc_ref)

    else:
        out_ref, fwd_ref, bwd_ref, wide = rest
    for k in range(pb):
        part = p_ref[k].astype(jnp.float32)
        for j in range(v_ref.shape[1]):
            q = part * t_ref[j]
            new = stencil(
                y0,
                v_ref[k, j].astype(jnp.float32),
                lo_ref[k, j].astype(jnp.float32),
                hi_ref[k, j].astype(jnp.float32),
                q,
                c_ref,
                wide,
            )
            if final:
                shift = (0.5 * coupling) * m_ref[pl.program_id(0) * pb + k, j]
                acc_ref[j] = acc_ref[j] - (new - shift) * part
            else:
                out_ref[k, j] = new
                fwd_ref[k, j] = new[row_count - halo : row_count].astype(jnp.bfloat16)
                bwd_ref[k, j] = new[0:halo].astype(jnp.bfloat16)


def sweep_call(final, v, from_warm, lo, hi, partner, targets, tmat, scalars, means=None, init=None):
    orb, tgt, halo, width = lo.shape
    row_count = targets.shape[1]
    pb = PER_STEP
    if from_warm:
        v_spec = pl.BlockSpec(
            (None, pb, tgt, row_count, width), lambda i, sc: (sc[1], i, 0, 0, 0)
        )
    else:
        v_spec = pl.BlockSpec((pb, tgt, row_count, width), lambda i, sc: (i, 0, 0, 0))
    h_spec = pl.BlockSpec((pb, tgt, halo, width), lambda i, sc: (i, 0, 0, 0))
    p_spec = pl.BlockSpec((pb, row_count, width), lambda i, sc: (sc[2] // pb + i, 0, 0))
    t_spec = pl.BlockSpec((tgt, row_count, width), lambda i, sc: (0, 0, 0))
    c_spec = pl.BlockSpec((width, width), lambda i, sc: (0, 0))
    cells = orb * tgt * row_count * width
    in_specs = [v_spec, h_spec, h_spec, p_spec, t_spec, c_spec]
    extra = []
    if final:
        in_specs.append(pl.BlockSpec(memory_space=pltpu.SMEM))
        extra.append(means)
        if init is not None:
            in_specs.append(pl.BlockSpec((tgt, row_count, width), lambda i, sc: (0, 0, 0)))
            extra.append(init)
        out_shape = jax.ShapeDtypeStruct((tgt, row_count, width), jnp.float32)
        out_specs = pl.BlockSpec((tgt, row_count, width), lambda i, sc: (0, 0, 0))
        out_bytes = tgt * row_count * width * 4
    else:
        out_shape = (
            jax.ShapeDtypeStruct((orb, tgt, row_count, width), jnp.float32),
            jax.ShapeDtypeStruct((orb, tgt, halo, width), jnp.bfloat16),
            jax.ShapeDtypeStruct((orb, tgt, halo, width), jnp.bfloat16),
        )
        out_specs = (
            pl.BlockSpec((pb, tgt, row_count, width), lambda i, sc: (i, 0, 0, 0)),
            h_spec,
            h_spec,
        )
        out_bytes = cells * 4 + 2 * orb * tgt * halo * width * 2
    in_bytes = (
        cells * v.dtype.itemsize
        + 2 * orb * tgt * halo * width * 2
        + orb * row_count * width * 2
        + tgt * row_count * width * 4
    )
    grid_spec = pltpu.PrefetchScalarGridSpec(
        num_scalar_prefetch=1,
        grid=(orb // pb,),
        in_specs=in_specs,
        out_specs=out_specs,
        scratch_shapes=[pltpu.VMEM((row_count + 2 * halo, width), jnp.float32)],
    )
    return pl.pallas_call(
        functools.partial(sweep_kernel, final, init is not None),
        grid_spec=grid_spec,
        out_shape=out_shape,
        compiler_params=pltpu.CompilerParams(dimension_semantics=("arbitrary",)),
        cost_estimate=pl.CostEstimate(
            flops=cells * (4 * width + 24),
            transcendentals=0,
            bytes_accessed=in_bytes + out_bytes,
        ),
    )(scalars, v, lo, hi, partner, targets, tmat, *extra)


def exchange_halos(fwd, bwd):
    count = lax.axis_size("domain")
    forward = [(k, (k + 1) % count) for k in range(count)]
    backward = [((k + 1) % count, k) for k in range(count)]
    return lax.ppermute(fwd, "domain", forward), lax.ppermute(bwd, "domain", backward)


def warm_halos(warm_start, s, row_count):
    warm_block = lax.dynamic_index_in_dim(warm_start, s, 0, keepdims=False)
    return warm_block[:, :, row_count - GY :], warm_block[:, :, :GY]


def finish_stream(potential, fwd, bwd, partner, targets, tmat, scalars, means, init):
    for sweep_index in range(1, SWEEPS - 1):
        lo, hi = exchange_halos(fwd, bwd)
        potential, fwd, bwd = sweep_call(
            False, potential, False, lo, hi, partner, targets, tmat, scalars
        )
    lo, hi = exchange_halos(fwd, bwd)
    return sweep_call(
        True, potential, False, lo, hi, partner, targets, tmat, scalars, means, init
    )


def butterfly_sum(x, axis):
    count = lax.axis_size(axis)
    step = 1
    while step < count:
        radix = 2
        total = x
        for part in range(1, radix):
            pairs = [
                (k, (k // (step * radix)) * step * radix + ((k // step) % radix ^ part) * step + k % step)
                for k in range(count)
            ]
            total = total + lax.ppermute(x, axis, pairs)
        x = total
        step *= radix
    return x


def swap_over_y(block, mesh_shape):
    bands, domains = mesh_shape
    lanes = domains // 2
    def index(y, rest):
        return (y // 2) * domains + (y % 2) * lanes + rest
    ring = 2 * bands
    def shift(direction):
        return [
            (index(y, rest), index((y + direction) % ring, rest))
            for y in range(ring)
            for rest in range(lanes)
        ]
    half = block.shape[0] // 2
    axes = ("band", "domain")
    plus = lax.ppermute(block[:half], axes, shift(1))
    minus = lax.ppermute(block[half:], axes, shift(-1))
    return plus, minus, lambda plus, minus: jnp.concatenate(
        [lax.ppermute(plus, axes, shift(1)), lax.ppermute(minus, axes, shift(-1))], axis=0
    )


def pair_sums(block, targets):
    part = block.astype(jnp.float32)
    return jnp.sum(part[:, None] * targets[None], axis=(2, 3))


def body(targets, partner_pool, owners, warm_start):
    row_count = targets.shape[1]
    cell_count = GX * GY * GZ
    domain = lax.axis_index("domain")
    band = lax.axis_index("band")
    y0 = (domain * row_count) % GY
    s_own = jnp.where(owners[0] == band, 0, 1).astype(jnp.int32)
    s_rem = 1 - s_own
    own_block = lax.dynamic_slice_in_dim(partner_pool, s_own * ORB, ORB, 0)
    tmat = circulant(targets.shape[2])
    own_scalars = jnp.stack([y0, s_own, s_own * ORB]).astype(jnp.int32)
    rem_scalars = jnp.stack([y0, s_rem, jnp.zeros((), jnp.int32)]).astype(jnp.int32)

    own_halos = exchange_halos(*warm_halos(warm_start, s_own, row_count))
    plus, minus, finish_swap = swap_over_y(
        own_block, (lax.axis_size("band"), lax.axis_size("domain"))
    )
    rem_sends, own_halos, plus, minus = lax.optimization_barrier(
        (warm_halos(warm_start, s_rem, row_count), own_halos, plus, minus)
    )
    rem_halos = exchange_halos(*rem_sends)
    rem_block = finish_swap(plus, minus)
    potential, fwd, bwd = sweep_call(
        False, warm_start, True, *own_halos, partner_pool, targets, tmat, own_scalars
    )
    rem_state = sweep_call(
        False, warm_start, True, *rem_halos, rem_block, targets, tmat, rem_scalars
    )

    sums = jnp.stack([pair_sums(own_block, targets), pair_sums(rem_block, targets)])
    means = butterfly_sum(sums, "domain") / cell_count

    own_acc = finish_stream(
        potential, fwd, bwd, partner_pool, targets, tmat, own_scalars, means[0], None
    )
    return finish_stream(
        *rem_state, rem_block, targets, tmat, rem_scalars, means[1], own_acc
    )


def solution(mesh):
    return jax.shard_map(
        body,
        mesh=mesh,
        in_specs=(
            P("band", "domain", None),
            P("band", "domain", None),
            P(),
            P(None, None, "band", "domain", None),
        ),
        out_specs=P("band", "domain", None),
        check_vma=False,
    )
```
